32 devices in a mesh: tile: 8 (over y, x, core), member: 4 (over z).
Axes of the slice: x: 2, y: 2, z: 4, core: 2. Of those that a mesh axis runs over, the one named last changes fastest.
Arguments:
- alpha: float32 [12, 256, 2048], P('member', None, 'tile'), may hold values from -6 to 6
- ensemble: bfloat16 [12, 256, 3, 2048], P('member', None, None, 'tile'), may hold values from -4 to 4
- background: float32 [256, 3, 2048], P(None, None, 'tile'), may hold values from -6 to 6
- measured_values: float32 [256, 3, 2048], P(None, None, 'tile'), may hold values from -6 to 6
- precision_factor: float32 [256, 3, 2048], P(None, None, 'tile'), may hold values from 0.3 to 3
- depth: float32 [256, 2048], P(None, 'tile'), may hold values from 0.5 to 2
- loc_cols: float32 [256, 256], replicated
- loc_rows: float32 [256, 256], replicated
Outputs:
- cost_derivative: float32 [12, 256, 2048], P('member', None, 'tile')
- predicted_final: float32 [256, 3, 2048], P('member', None, 'tile')
The draws below stay inside these ranges and needn't reach their ends.
All inputs are finite; a program needn't handle non-finite values.
Results may differ from the reference program's by a relative error of at most 0.0003.
Values sent between devices are 32-bit elements; how exact they have to be, the bound alone decides.
No kernel may reach another device: no remote copies, remote signals or barrier semaphores. Data moves between devices by JAX's collectives and lax.ppermute only.
A program may use at most 64 MiB of HBM per device.

```python
import math
import jax
import jax.numpy as jnp
from jax import lax

LOC = 256
MEM_DEV = 3
STEPS = 2
ENS = 12
NROW = 2048
N_TILE = 8
N_MEMBER = 4


def loc_table(key):
    position = jnp.arange(LOC, dtype=jnp.float32)
    offset = position[:, None] - position[None, :]
    scale_len = LOC / 8.0
    envelope = jnp.exp(-0.5 * (offset / scale_len) ** 2)
    roughness = jax.random.uniform(key, (LOC, LOC), jnp.float32, 0.6, 1.4)
    return envelope * roughness / jnp.sqrt(scale_len)


def draw_loc_cols(key, part):
    return loc_table(jax.random.fold_in(key, 11))


def draw_loc_rows(key, part):
    return loc_table(jax.random.fold_in(key, 23))


def strengthened(array, key, source, target, shards_of, factor):
    def block_of(dim):
        return (jnp.arange(array.shape[dim]) // (array.shape[dim] // shards_of)).reshape((-1,) + (1,) * (array.ndim - 1 - dim))

    first = jax.random.permutation(key, shards_of)[block_of(target)]
    second = (block_of(target) + shards_of // 2) % shards_of
    return jnp.where((block_of(source) == first) | (block_of(source) == second), factor * array, array)


def levels(stream_key, extent, shards, least, top_value):
    def one(dim, parts):
        steps = jax.random.uniform(jax.random.fold_in(jax.random.fold_in(stream_key, 6), dim), (parts,), jnp.float32, least / len(shards), top_value / len(shards))
        return jnp.repeat(jnp.exp(steps), extent[dim] // parts).reshape((-1,) + (1,) * (len(extent) - dim - 1))

    level = one(*shards[0])
    for cut in shards[1:]:
        level = level * one(*cut)
    return level


def bell_draw(rng, dims, spread, reach, pieces=(), kind=jnp.bfloat16):
    values = jax.random.normal(rng, dims, jnp.float32) * spread
    if len(pieces) > 0:
        values = levels(rng, dims, pieces, -0.22, 0.18) * values
    return jnp.clip(values, min=-reach, max=reach).astype(kind)


def heavy_noise(key, extent, width, most, shards, heavy, kind=jnp.bfloat16):
    result = width * jax.random.normal(key, extent, jnp.float32)
    if shards:
        result = result * levels(key, extent, shards, -0.22, 0.18)
    return jnp.clip(strengthened(result, jax.random.fold_in(key, 3), *heavy), -most, most).astype(kind)


def setup_inputs(seed: int = 0) -> dict:
    streams_of = jax.random.split(jax.random.key(seed), 9)
    return {
        "alpha": bell_draw(streams_of[0], (ENS, LOC, NROW), 1.0, 6.0, ((0, 4), (2, 8)), jnp.float32),
        "ensemble": heavy_noise(streams_of[1], (ENS, LOC, 3, NROW), (0.7 / (MEM_DEV * N_MEMBER) ** 0.5), 4.0, ((0, 4), (3, 8)), (0, 1, 4, 2.0)),
        "background": bell_draw(streams_of[2], (LOC, 3, NROW), 1.0, 6.0, ((2, 8),), jnp.float32),
        "measured_values": bell_draw(streams_of[3], (LOC, 3, NROW), 1.0, 6.0, ((2, 8),), jnp.float32),
        "precision_factor": jnp.clip(jnp.exp(math.log(3.0) - 2.3025851 * jax.random.uniform(streams_of[4], (LOC, 3, NROW), jnp.float32) ** levels(streams_of[4], (LOC, 3, NROW), ((2, 8),), -0.2, 0.2)), 0.3, 3.0),
        "depth": jnp.clip(jnp.exp(math.log(2.0) - 1.3862944 * jax.random.uniform(streams_of[5], (LOC, NROW), jnp.float32) ** levels(streams_of[5], (LOC, NROW), ((1, 8),), -0.2, 0.2)), 0.5, 2.0),
        "loc_cols": draw_loc_cols(jax.random.fold_in(streams_of[8], 71), 0),
        "loc_rows": draw_loc_rows(jax.random.fold_in(streams_of[8], 71), 0),
    }


COURANT = 0.3

def col_slope(field):
    return 0.5 * (jnp.roll(field, -1, 0) - jnp.roll(field, 1, 0))

def row_slope(field):
    return 0.5 * (jnp.roll(field, -1, 2) - jnp.roll(field, 1, 2))

def reference(alpha, ensemble, background, measured_values, precision_factor, depth, loc_cols, loc_rows):
    highest = lax.Precision.HIGHEST

    def localize(control):
        blocks = control.reshape(LOC, N_TILE, LOC)
        rows_done = jnp.einsum('ctr,qr->ctq', blocks, loc_rows, precision=highest)
        return jnp.einsum('cd,dtq->ctq', loc_cols, rows_done, precision=highest).reshape(LOC, NROW)

    def localize_adjoint(projected):
        blocks = projected.reshape(LOC, N_TILE, LOC)
        rows_done = jnp.einsum('ctr,rq->ctq', blocks, loc_rows, precision=highest)
        return jnp.einsum('cd,ctq->dtq', loc_cols, rows_done, precision=highest).reshape(LOC, NROW)

    def add_member(total, item):
        control, member_pert = item
        localized = localize(control)
        return (total + member_pert.astype(jnp.float32) * localized[:, None, :], None)
    increment, unused = lax.scan(add_member, jnp.zeros((LOC, 3, NROW), jnp.float32), (alpha, ensemble))
    initial_state = background + increment
    depth3_triple = depth[:, None, :]
    free_elevation = initial_state[:, 0:1]
    current_speed = initial_state[:, 1:3]
    for repeat in range(STEPS):
        free_elevation = free_elevation - COURANT * depth3_triple * (col_slope(current_speed[:, 0:1]) + row_slope(current_speed[:, 1:2]))
        current_speed = current_speed - COURANT * jnp.concatenate([col_slope(free_elevation), row_slope(free_elevation)], axis=1)
    predicted_final = jnp.concatenate([free_elevation, current_speed], axis=1)
    residual_difference = precision_factor * (predicted_final - measured_values)
    adj_height = residual_difference[:, 0:1]
    adj_velocity = residual_difference[:, 1:3]
    for repeat in range(STEPS):
        summed = adj_height + COURANT * (col_slope(adj_velocity[:, 0:1]) + row_slope(adj_velocity[:, 1:2]))
        weighted = depth3_triple * summed
        adj_velocity = adj_velocity + COURANT * jnp.concatenate([col_slope(weighted), row_slope(weighted)], axis=1)
        adj_height = summed
    backward_pass = jnp.concatenate([adj_height, adj_velocity], axis=1)

    def member_grad(carry, item):
        control, member_pert = item
        projected = lax.optimization_barrier(jnp.sum(member_pert.astype(jnp.float32) * backward_pass, axis=1))
        return (carry, control + localize_adjoint(projected))
    unused, cost_derivative = lax.scan(member_grad, jnp.zeros((), jnp.float32), (alpha, ensemble))
    return (cost_derivative, predicted_final)
```

```python
import jax
import jax.numpy as jnp
from jax import lax
from jax.sharding import PartitionSpec as P

STEPS = 2
COURANT = 0.3
HALO = 4 * STEPS


def shift_rows(x, sides):
    count = lax.axis_size("tile")
    up = [(i, (i + 1) % count) for i in range(count)]
    down = [(j, i) for i, j in up]
    lo, hi = sides
    before = lax.ppermute(hi, "tile", up)
    after = lax.ppermute(lo, "tile", down)
    return before, after


def col_slope(f):
    return 0.5 * (jnp.roll(f, -1, 0) - jnp.roll(f, 1, 0))


def row_slope(f):
    return 0.5 * (jnp.roll(f, -1, 1) - jnp.roll(f, 1, 1))


def dynamics(h, u, v, dep, prec, meas):
    for _ in range(STEPS):
        h = h - COURANT * dep * (col_slope(u) + row_slope(v))
        u = u - COURANT * col_slope(h)
        v = v - COURANT * row_slope(h)
    pred = (h, u, v)
    a, p, q = (prec[i] * (pred[i] - meas[i]) for i in range(3))
    for _ in range(STEPS):
        e = a + COURANT * (col_slope(p) + row_slope(q))
        w = dep * e
        p = p + COURANT * col_slope(w)
        q = q + COURANT * row_slope(w)
        a = e
    return pred, (a, p, q)


def body(alpha, ensemble, background, measured_values, precision_factor, depth, loc_cols, loc_rows):
    highest = lax.Precision.HIGHEST
    ncol, nfield, nrow = background.shape
    block_cols = ncol // lax.axis_size("member")
    col_start = lax.axis_index("member") * block_cols

    inputs = jnp.concatenate(
        [background, measured_values, precision_factor, depth[:, None, :]], axis=1
    )
    in_before, in_after = shift_rows(inputs, (inputs[:, :, :HALO], inputs[:, :, -HALO:]))

    localized = jnp.einsum("cd,kdr->kcr", loc_cols, alpha, precision=highest)
    localized = jnp.einsum("kcr,qr->kcq", localized, loc_rows, precision=highest)
    ens = ensemble.astype(jnp.float32)
    partial = jnp.sum(ens * localized[:, :, None, :], axis=0).transpose(1, 0, 2)
    p_before, p_after = shift_rows(partial, (partial[:, :, :HALO], partial[:, :, -HALO:]))
    halo = jnp.concatenate([p_before, p_after], axis=2).transpose(0, 2, 1)
    summed = lax.psum(jnp.concatenate([partial, halo], axis=1), "member")
    incr_main = summed[:, :ncol]
    incr_halo = summed[:, ncol:].transpose(0, 2, 1)
    incr = jnp.concatenate(
        [incr_halo[:, :, :HALO], incr_main, incr_halo[:, :, HALO:]], axis=2
    )
    ext = jnp.concatenate([in_before, inputs, in_after], axis=2)

    state = [ext[:, i] + incr[i] for i in range(nfield)]
    meas = [ext[:, nfield + i] for i in range(nfield)]
    prec = [ext[:, 2 * nfield + i] for i in range(nfield)]
    dep = ext[:, 3 * nfield]
    pred, adj = dynamics(*state, dep, prec, meas)

    inner = slice(HALO, HALO + nrow)
    pred = jnp.stack([f[:, inner] for f in pred], axis=1)
    predicted_final = lax.dynamic_slice_in_dim(pred, col_start, block_cols, 0)
    adj = jnp.stack([f[:, inner] for f in adj], axis=1)
    projected = jnp.sum(ens * adj[None], axis=2)
    rows_done = jnp.einsum("knr,rq->knq", projected, loc_rows, precision=highest)
    cost_derivative = alpha + jnp.einsum("cd,kcq->kdq", loc_cols, rows_done, precision=highest)
    return (cost_derivative, predicted_final)


def solution(mesh):
    return jax.shard_map(
        body,
        mesh=mesh,
        in_specs=(
            P("member", None, "tile"),
            P("member", None, None, "tile"),
            P(None, None, "tile"),
            P(None, None, "tile"),
            P(None, None, "tile"),
            P(None, "tile"),
            P(),
            P(),
        ),
        out_specs=(P("member", None, "tile"), P("member", None, "tile")),
        check_vma=False,
    )
```

```python
import jax
import jax.numpy as jnp
from jax import lax
from jax.sharding import PartitionSpec as P

STEPS = 2
COURANT = 0.3
HALO = 4 * STEPS


def shift_rows(x, sides):
    count = lax.axis_size("tile")
    up = [(i, (i + 1) % count) for i in range(count)]
    down = [(j, i) for i, j in up]
    lo, hi = sides
    before = lax.ppermute(hi, "tile", up)
    after = lax.ppermute(lo, "tile", down)
    return before, after


def col_slope(f):
    return 0.5 * (jnp.roll(f, -1, 0) - jnp.roll(f, 1, 0))


def row_slope(f):
    return 0.5 * (jnp.roll(f, -1, 1) - jnp.roll(f, 1, 1))


def dynamics(h, u, v, dep, prec, meas):
    for _ in range(STEPS):
        h = h - COURANT * dep * (col_slope(u) + row_slope(v))
        u = u - COURANT * col_slope(h)
        v = v - COURANT * row_slope(h)
    pred = (h, u, v)
    a, p, q = (prec[i] * (pred[i] - meas[i]) for i in range(3))
    for _ in range(STEPS):
        e = a + COURANT * (col_slope(p) + row_slope(q))
        w = dep * e
        p = p + COURANT * col_slope(w)
        q = q + COURANT * row_slope(w)
        a = e
    return pred, (a, p, q)


def member_sum(x):
    count = lax.axis_size("member")
    me = lax.axis_index("member")
    rows, lanes = x.shape
    piece = -(-rows // (8 * count)) * 8
    x = jnp.pad(x, ((0, piece * count - rows), (0, 0))).reshape(count, piece, lanes)
    acc = lax.dynamic_index_in_dim(x, me, 0, keepdims=False)
    for s in range(1, count):
        shift = [(i, (i + s) % count) for i in range(count)]
        sent = lax.dynamic_index_in_dim(x, (me + s) % count, 0, keepdims=False)
        acc = acc + lax.ppermute(sent, "member", shift)
    out = jnp.zeros_like(x)
    out = lax.dynamic_update_index_in_dim(out, acc, me, 0)
    for s in range(1, count):
        shift = [(i, (i + s) % count) for i in range(count)]
        got = lax.ppermute(acc, "member", shift)
        out = lax.dynamic_update_index_in_dim(out, got, (me + count - s) % count, 0)
    return out.reshape(piece * count, lanes)[:rows]


def body(alpha, ensemble, background, measured_values, precision_factor, depth, loc_cols, loc_rows):
    highest = lax.Precision.HIGHEST
    ncol, nfield, nrow = background.shape
    block_cols = ncol // lax.axis_size("member")
    col_start = lax.axis_index("member") * block_cols

    inputs = jnp.concatenate(
        [background, measured_values, precision_factor, depth[:, None, :]], axis=1
    )
    localized = jnp.einsum("cd,kdr->kcr", loc_cols, alpha, precision=highest)
    localized = jnp.einsum("kcr,qr->kcq", localized, loc_rows, precision=highest)
    ens = ensemble.astype(jnp.float32)
    partial = jnp.sum(ens * localized[:, :, None, :], axis=0)
    both = jnp.concatenate([partial, inputs], axis=1)
    before, after = shift_rows(both, (both[:, :, :HALO], both[:, :, -HALO:]))
    halo = jnp.concatenate([before[:, :nfield], after[:, :nfield]], axis=2).transpose(1, 2, 0)
    flat = jnp.concatenate(
        [partial.transpose(1, 0, 2).reshape(nfield * ncol, nrow),
         halo.reshape(nfield * 2 * HALO, ncol)], axis=0)
    summed = member_sum(flat)
    incr_main = summed[: nfield * ncol].reshape(nfield, ncol, nrow)
    incr_halo = summed[nfield * ncol:].reshape(nfield, 2 * HALO, ncol).transpose(0, 2, 1)
    incr = jnp.concatenate(
        [incr_halo[:, :, :HALO], incr_main, incr_halo[:, :, HALO:]], axis=2
    )
    ext = jnp.concatenate([before[:, nfield:], inputs, after[:, nfield:]], axis=2)

    state = [ext[:, i] + incr[i] for i in range(nfield)]
    meas = [ext[:, nfield + i] for i in range(nfield)]
    prec = [ext[:, 2 * nfield + i] for i in range(nfield)]
    dep = ext[:, 3 * nfield]
    pred, adj = dynamics(*state, dep, prec, meas)

    inner = slice(HALO, HALO + nrow)
    pred = jnp.stack([f[:, inner] for f in pred], axis=1)
    predicted_final = lax.dynamic_slice_in_dim(pred, col_start, block_cols, 0)
    adj = jnp.stack([f[:, inner] for f in adj], axis=1)
    projected = jnp.sum(ens * adj[None], axis=2)
    rows_done = jnp.einsum("knr,rq->knq", projected, loc_rows, precision=highest)
    cost_derivative = alpha + jnp.einsum("cd,kcq->kdq", loc_cols, rows_done, precision=highest)
    return (cost_derivative, predicted_final)


def solution(mesh):
    return jax.shard_map(
        body,
        mesh=mesh,
        in_specs=(
            P("member", None, "tile"),
            P("member", None, None, "tile"),
            P(None, None, "tile"),
            P(None, None, "tile"),
            P(None, None, "tile"),
            P(None, "tile"),
            P(),
            P(),
        ),
        out_specs=(P("member", None, "tile"), P("member", None, "tile")),
        check_vma=False,
    )
```

```python
import jax
import jax.numpy as jnp
from jax import lax
from jax.sharding import PartitionSpec as P

STEPS = 2
COURANT = 0.3
HALO = 4 * STEPS


def shift_rows(x, sides):
    count = lax.axis_size("tile")
    up = [(i, (i + 1) % count) for i in range(count)]
    down = [(j, i) for i, j in up]
    lo, hi = sides
    before = lax.ppermute(hi, "tile", up)
    after = lax.ppermute(lo, "tile", down)
    return before, after


def col_slope(f):
    return 0.5 * (jnp.roll(f, -1, 0) - jnp.roll(f, 1, 0))


def row_slope(f):
    return 0.5 * (jnp.roll(f, -1, 1) - jnp.roll(f, 1, 1))


def dynamics(h, u, v, dep, prec, meas):
    for _ in range(STEPS):
        h = h - COURANT * dep * (col_slope(u) + row_slope(v))
        u = u - COURANT * col_slope(h)
        v = v - COURANT * row_slope(h)
    pred = (h, u, v)
    a, p, q = (prec[i] * (pred[i] - meas[i]) for i in range(3))
    for _ in range(STEPS):
        e = a + COURANT * (col_slope(p) + row_slope(q))
        w = dep * e
        p = p + COURANT * col_slope(w)
        q = q + COURANT * row_slope(w)
        a = e
    return pred, (a, p, q)


def member_sum(x):
    count = lax.axis_size("member")
    me = lax.axis_index("member")
    rows, lanes = x.shape
    piece = -(-rows // (8 * count)) * 8
    x = jnp.pad(x, ((0, piece * count - rows), (0, 0))).reshape(count, piece, lanes)
    acc = lax.dynamic_index_in_dim(x, me, 0, keepdims=False)
    for s in range(1, count):
        shift = [(i, (i + s) % count) for i in range(count)]
        sent = lax.dynamic_index_in_dim(x, (me + s) % count, 0, keepdims=False)
        acc = acc + lax.ppermute(sent, "member", shift)
    out = jnp.zeros_like(x)
    out = lax.dynamic_update_index_in_dim(out, acc, me, 0)
    for s in range(1, count):
        shift = [(i, (i + s) % count) for i in range(count)]
        got = lax.ppermute(acc, "member", shift)
        out = lax.dynamic_update_index_in_dim(out, got, (me + count - s) % count, 0)
    return out.reshape(piece * count, lanes)[:rows]


def member_gather_sum(x):
    count = lax.axis_size("member")
    me = lax.axis_index("member")
    pieces = jnp.zeros((count,) + x.shape, x.dtype)
    pieces = lax.dynamic_update_index_in_dim(pieces, x, me, 0)
    for s in range(1, count):
        shift = [(i, (i + s) % count) for i in range(count)]
        got = lax.ppermute(x, "member", shift)
        pieces = lax.dynamic_update_index_in_dim(pieces, got, (me + count - s) % count, 0)
    total = pieces[0]
    for i in range(1, count):
        total = total + pieces[i]
    return total


def body(alpha, ensemble, background, measured_values, precision_factor, depth, loc_cols, loc_rows):
    highest = lax.Precision.HIGHEST
    ncol, nfield, nrow = background.shape
    block_cols = ncol // lax.axis_size("member")
    col_start = lax.axis_index("member") * block_cols

    localized = jnp.einsum("cd,kdr->kcr", loc_cols, alpha, precision=highest)
    localized = jnp.einsum("kcr,qr->kcq", localized, loc_rows, precision=highest)
    ens = ensemble.astype(jnp.float32)
    partial = jnp.sum(ens * localized[:, :, None, :], axis=0)

    def edge(part):
        return jnp.concatenate(
            [partial[:, :, part], background[:, :, part], measured_values[:, :, part],
             precision_factor[:, :, part], depth[:, None, part]], axis=1)

    before, after = shift_rows(None, (edge(slice(0, HALO)), edge(slice(nrow - HALO, nrow))))
    summed = member_sum(partial.transpose(1, 0, 2).reshape(nfield * ncol, nrow))
    incr_main = summed.reshape(nfield, ncol, nrow)
    halo = member_gather_sum(jnp.concatenate([before[:, :nfield], after[:, :nfield]], axis=2))

    def extend(main, lo, hi):
        return jnp.concatenate([lo, main, hi], axis=1)

    state = [extend(background[:, i] + incr_main[i],
                    before[:, nfield + i] + halo[:, i, :HALO],
                    after[:, nfield + i] + halo[:, i, HALO:]) for i in range(nfield)]
    meas = [extend(measured_values[:, i], before[:, 2 * nfield + i], after[:, 2 * nfield + i])
            for i in range(nfield)]
    prec = [extend(precision_factor[:, i], before[:, 3 * nfield + i], after[:, 3 * nfield + i])
            for i in range(nfield)]
    dep = extend(depth, before[:, 4 * nfield], after[:, 4 * nfield])
    pred, adj = dynamics(*state, dep, prec, meas)

    inner = slice(HALO, HALO + nrow)
    pred = jnp.stack([f[:, inner] for f in pred], axis=1)
    predicted_final = lax.dynamic_slice_in_dim(pred, col_start, block_cols, 0)
    adj = jnp.stack([f[:, inner] for f in adj], axis=1)
    projected = jnp.sum(ens * adj[None], axis=2)
    rows_done = jnp.einsum("knr,rq->knq", projected, loc_rows, precision=highest)
    cost_derivative = alpha + jnp.einsum("cd,kcq->kdq", loc_cols, rows_done, precision=highest)
    return (cost_derivative, predicted_final)


def solution(mesh):
    return jax.shard_map(
        body,
        mesh=mesh,
        in_specs=(
            P("member", None, "tile"),
            P("member", None, None, "tile"),
            P(None, None, "tile"),
            P(None, None, "tile"),
            P(None, None, "tile"),
            P(None, "tile"),
            P(),
            P(),
        ),
        out_specs=(P("member", None, "tile"), P("member", None, "tile")),
        check_vma=False,
    )
```

```python
import jax
import jax.numpy as jnp
from jax import lax
from jax.sharding import PartitionSpec as P

STEPS = 2
COURANT = 0.3
HALO = 4 * STEPS


def shift_rows(x, sides):
    count = lax.axis_size("tile")
    up = [(i, (i + 1) % count) for i in range(count)]
    down = [(j, i) for i, j in up]
    lo, hi = sides
    before = lax.ppermute(hi, "tile", up)
    after = lax.ppermute(lo, "tile", down)
    return before, after


def col_slope(f):
    return 0.5 * (jnp.roll(f, -1, 0) - jnp.roll(f, 1, 0))


def row_slope(f):
    return 0.5 * (jnp.roll(f, -1, 1) - jnp.roll(f, 1, 1))


def dynamics(h, u, v, dep, prec, meas):
    for _ in range(STEPS):
        h = h - COURANT * dep * (col_slope(u) + row_slope(v))
        u = u - COURANT * col_slope(h)
        v = v - COURANT * row_slope(h)
    pred = (h, u, v)
    a, p, q = (prec[i] * (pred[i] - meas[i]) for i in range(3))
    for _ in range(STEPS):
        e = a + COURANT * (col_slope(p) + row_slope(q))
        w = dep * e
        p = p + COURANT * col_slope(w)
        q = q + COURANT * row_slope(w)
        a = e
    return pred, (a, p, q)


def member_sum(x):
    count = lax.axis_size("member")
    me = lax.axis_index("member")
    rows, lanes = x.shape
    piece = -(-rows // (8 * count)) * 8
    x = jnp.pad(x, ((0, piece * count - rows), (0, 0))).reshape(count, piece, lanes)
    acc = lax.dynamic_index_in_dim(x, me, 0, keepdims=False)
    for s in range(1, count):
        shift = [(i, (i + s) % count) for i in range(count)]
        sent = lax.dynamic_index_in_dim(x, (me + s) % count, 0, keepdims=False)
        acc = acc + lax.ppermute(sent, "member", shift)
    out = jnp.zeros_like(x)
    out = lax.dynamic_update_index_in_dim(out, acc, me, 0)
    for s in range(1, count):
        shift = [(i, (i + s) % count) for i in range(count)]
        got = lax.ppermute(acc, "member", shift)
        out = lax.dynamic_update_index_in_dim(out, got, (me + count - s) % count, 0)
    return out.reshape(piece * count, lanes)[:rows]


def member_gather_sum(x):
    count = lax.axis_size("member")
    me = lax.axis_index("member")
    pieces = [None] * count
    pieces[0] = x
    for s in range(1, count):
        shift = [(i, (i + s) % count) for i in range(count)]
        pieces[s] = lax.ppermute(x, "member", shift)
    total = None
    for src in range(count):
        term = pieces[0]
        for s in range(1, count):
            term = jnp.where((me + count - s) % count == src, pieces[s], term)
        total = term if total is None else total + term
    return total


def body(alpha, ensemble, background, measured_values, precision_factor, depth, loc_cols, loc_rows):
    highest = lax.Precision.HIGHEST
    ncol, nfield, nrow = background.shape
    block_cols = ncol // lax.axis_size("member")
    col_start = lax.axis_index("member") * block_cols

    inputs = jnp.concatenate(
        [background, measured_values, precision_factor, depth[:, None, :]], axis=1
    )
    mem = alpha.shape[0]
    cols_b = jnp.broadcast_to(loc_cols, (mem,) + loc_cols.shape)
    rows_b = jnp.broadcast_to(loc_rows, (mem,) + loc_rows.shape)
    def batched(lhs_dim, rhs_dim):
        return (((lhs_dim,), (rhs_dim,)), ((0,), (0,)))

    localized = lax.dot_general(cols_b, alpha, batched(2, 1), precision=highest)
    localized = lax.dot_general(localized, rows_b, batched(2, 2), precision=highest)
    ens = ensemble.astype(jnp.float32)
    partial = jnp.sum(ens * localized[:, :, None, :], axis=0)
    both = jnp.concatenate([partial, inputs], axis=1)
    before, after = shift_rows(
        None, (both[:, :, :HALO].transpose(1, 2, 0), both[:, :, -HALO:].transpose(1, 2, 0)))
    halo = jnp.concatenate([before[:nfield], after[:nfield]], axis=1)
    before = before.transpose(2, 0, 1)
    after = after.transpose(2, 0, 1)
    summed = member_sum(partial.transpose(1, 0, 2).reshape(nfield * ncol, nrow))
    incr_main = summed.reshape(nfield, ncol, nrow)
    incr_halo = member_gather_sum(halo).transpose(0, 2, 1)
    incr = jnp.concatenate(
        [incr_halo[:, :, :HALO], incr_main, incr_halo[:, :, HALO:]], axis=2
    )
    ext = jnp.concatenate([before[:, nfield:], inputs, after[:, nfield:]], axis=2)

    state = [ext[:, i] + incr[i] for i in range(nfield)]
    meas = [ext[:, nfield + i] for i in range(nfield)]
    prec = [ext[:, 2 * nfield + i] for i in range(nfield)]
    dep = ext[:, 3 * nfield]
    pred, adj = dynamics(*state, dep, prec, meas)

    inner = slice(HALO, HALO + nrow)
    pred = jnp.stack([f[:, inner] for f in pred], axis=1)
    predicted_final = lax.dynamic_slice_in_dim(pred, col_start, block_cols, 0)
    adj = jnp.stack([f[:, inner] for f in adj], axis=1)
    projected = jnp.sum(ens * adj[None], axis=2)
    rows_done = lax.dot_general(projected, rows_b, batched(2, 1), precision=highest)
    cost_derivative = alpha + lax.dot_general(cols_b, rows_done, batched(1, 1), precision=highest)
    return (cost_derivative, predicted_final)


def solution(mesh):
    return jax.shard_map(
        body,
        mesh=mesh,
        in_specs=(
            P("member", None, "tile"),
            P("member", None, None, "tile"),
            P(None, None, "tile"),
            P(None, None, "tile"),
            P(None, None, "tile"),
            P(None, "tile"),
            P(),
            P(),
        ),
        out_specs=(P("member", None, "tile"), P("member", None, "tile")),
        check_vma=False,
    )
```

```python
import jax
import jax.numpy as jnp
from jax import lax
from jax.sharding import PartitionSpec as P

STEPS = 2
COURANT = 0.3
HALO = 4 * STEPS


def shift_rows(x, sides):
    count = lax.axis_size("tile")
    up = [(i, (i + 1) % count) for i in range(count)]
    down = [(j, i) for i, j in up]
    lo, hi = sides
    before = lax.ppermute(hi, "tile", up)
    after = lax.ppermute(lo, "tile", down)
    return before, after


def col_slope(f):
    return 0.5 * (jnp.roll(f, -1, 0) - jnp.roll(f, 1, 0))


def row_slope(f):
    return 0.5 * (jnp.roll(f, -1, 1) - jnp.roll(f, 1, 1))


def dynamics(h, u, v, dep, prec, meas):
    for _ in range(STEPS):
        h = h - COURANT * dep * (col_slope(u) + row_slope(v))
        u = u - COURANT * col_slope(h)
        v = v - COURANT * row_slope(h)
    pred = (h, u, v)
    a, p, q = (prec[i] * (pred[i] - meas[i]) for i in range(3))
    for _ in range(STEPS):
        e = a + COURANT * (col_slope(p) + row_slope(q))
        w = dep * e
        p = p + COURANT * col_slope(w)
        q = q + COURANT * row_slope(w)
        a = e
    return pred, (a, p, q)


def member_scatter(x):
    count = lax.axis_size("member")
    me = lax.axis_index("member")
    rows, lanes = x.shape
    piece = -(-rows // (8 * count)) * 8
    x = jnp.pad(x, ((0, piece * count - rows), (0, 0))).reshape(count, piece, lanes)
    acc = lax.dynamic_index_in_dim(x, me, 0, keepdims=False)
    for s in range(1, count):
        shift = [(i, (i + s) % count) for i in range(count)]
        sent = lax.dynamic_index_in_dim(x, (me + s) % count, 0, keepdims=False)
        acc = acc + lax.ppermute(sent, "member", shift)
    return acc, jnp.zeros((rows,), x.dtype)


def member_gather(acc, like):
    count = lax.axis_size("member")
    me = lax.axis_index("member")
    out = jnp.zeros((count,) + acc.shape, acc.dtype)
    out = lax.dynamic_update_index_in_dim(out, acc, me, 0)
    for s in range(1, count):
        shift = [(i, (i + s) % count) for i in range(count)]
        got = lax.ppermute(acc, "member", shift)
        out = lax.dynamic_update_index_in_dim(out, got, (me + count - s) % count, 0)
    return out.reshape(count * acc.shape[0], acc.shape[1])[: like.shape[0]]


def member_gather_sum(x):
    count = lax.axis_size("member")
    me = lax.axis_index("member")
    pieces = [None] * count
    pieces[0] = x
    for s in range(1, count):
        shift = [(i, (i + s) % count) for i in range(count)]
        pieces[s] = lax.ppermute(x, "member", shift)
    total = None
    for src in range(count):
        term = pieces[0]
        for s in range(1, count):
            term = jnp.where((me + count - s) % count == src, pieces[s], term)
        total = term if total is None else total + term
    return total


def body(alpha, ensemble, background, measured_values, precision_factor, depth, loc_cols, loc_rows):
    highest = lax.Precision.HIGHEST
    ncol, nfield, nrow = background.shape
    block_cols = ncol // lax.axis_size("member")
    col_start = lax.axis_index("member") * block_cols

    inputs = jnp.concatenate(
        [background, measured_values, precision_factor, depth[:, None, :]], axis=1
    )
    mem = alpha.shape[0]
    cols_b = jnp.broadcast_to(loc_cols, (mem,) + loc_cols.shape)
    rows_b = jnp.broadcast_to(loc_rows, (mem,) + loc_rows.shape)
    def batched(lhs_dim, rhs_dim):
        return (((lhs_dim,), (rhs_dim,)), ((0,), (0,)))

    localized = lax.dot_general(cols_b, alpha, batched(2, 1), precision=highest)
    localized = lax.dot_general(localized, rows_b, batched(2, 2), precision=highest)
    ens = ensemble.astype(jnp.float32)
    partial = jnp.sum(ens * localized[:, :, None, :], axis=0)
    both = jnp.concatenate([partial, inputs], axis=1)
    scattered = member_scatter(partial.transpose(1, 0, 2).reshape(nfield * ncol, nrow))
    scattered, both = lax.optimization_barrier((scattered, both))
    before, after = shift_rows(
        None, (both[:, :, :HALO].transpose(1, 2, 0), both[:, :, -HALO:].transpose(1, 2, 0)))
    halo = jnp.concatenate([before[:nfield], after[:nfield]], axis=1)
    before = before.transpose(2, 0, 1)
    after = after.transpose(2, 0, 1)
    summed = member_gather(*scattered)
    incr_main = summed.reshape(nfield, ncol, nrow)
    incr_halo = member_gather_sum(halo).transpose(0, 2, 1)
    incr = jnp.concatenate(
        [incr_halo[:, :, :HALO], incr_main, incr_halo[:, :, HALO:]], axis=2
    )
    ext = jnp.concatenate([before[:, nfield:], inputs, after[:, nfield:]], axis=2)

    state = [ext[:, i] + incr[i] for i in range(nfield)]
    meas = [ext[:, nfield + i] for i in range(nfield)]
    prec = [ext[:, 2 * nfield + i] for i in range(nfield)]
    dep = ext[:, 3 * nfield]
    pred, adj = dynamics(*state, dep, prec, meas)

    inner = slice(HALO, HALO + nrow)
    pred = jnp.stack([f[:, inner] for f in pred], axis=1)
    predicted_final = lax.dynamic_slice_in_dim(pred, col_start, block_cols, 0)
    adj = jnp.stack([f[:, inner] for f in adj], axis=1)
    projected = jnp.sum(ens * adj[None], axis=2)
    rows_done = lax.dot_general(projected, rows_b, batched(2, 1), precision=highest)
    cost_derivative = alpha + lax.dot_general(cols_b, rows_done, batched(1, 1), precision=highest)
    return (cost_derivative, predicted_final)


def solution(mesh):
    return jax.shard_map(
        body,
        mesh=mesh,
        in_specs=(
            P("member", None, "tile"),
            P("member", None, None, "tile"),
            P(None, None, "tile"),
            P(None, None, "tile"),
            P(None, None, "tile"),
            P(None, "tile"),
            P(),
            P(),
        ),
        out_specs=(P("member", None, "tile"), P("member", None, "tile")),
        check_vma=False,
    )
```

```python
import jax
import jax.numpy as jnp
from jax import lax
from jax.sharding import PartitionSpec as P

STEPS = 2
COURANT = 0.3
HALO = 4 * STEPS


def shift_rows(x, sides):
    count = lax.axis_size("tile")
    up = [(i, (i + 1) % count) for i in range(count)]
    down = [(j, i) for i, j in up]
    lo, hi = sides
    before = lax.ppermute(hi, "tile", up)
    after = lax.ppermute(lo, "tile", down)
    return before, after


def col_slope(f):
    return 0.5 * (jnp.roll(f, -1, 0) - jnp.roll(f, 1, 0))


def row_slope(f):
    return 0.5 * (jnp.roll(f, -1, 1) - jnp.roll(f, 1, 1))


def dynamics(h, u, v, dep, prec, meas):
    for _ in range(STEPS):
        h = h - COURANT * dep * (col_slope(u) + row_slope(v))
        u = u - COURANT * col_slope(h)
        v = v - COURANT * row_slope(h)
    pred = (h, u, v)
    a, p, q = (prec[i] * (pred[i] - meas[i]) for i in range(3))
    for _ in range(STEPS):
        e = a + COURANT * (col_slope(p) + row_slope(q))
        w = dep * e
        p = p + COURANT * col_slope(w)
        q = q + COURANT * row_slope(w)
        a = e
    return pred, (a, p, q)


def member_scatter(x):
    count = lax.axis_size("member")
    me = lax.axis_index("member")
    rows, lanes = x.shape
    piece = -(-rows // (8 * count)) * 8
    x = jnp.pad(x, ((0, piece * count - rows), (0, 0))).reshape(count, piece, lanes)
    acc = lax.dynamic_index_in_dim(x, me, 0, keepdims=False)
    for s in range(1, count):
        shift = [(i, (i + s) % count) for i in range(count)]
        sent = lax.dynamic_index_in_dim(x, (me + s) % count, 0, keepdims=False)
        acc = acc + lax.ppermute(sent, "member", shift)
    return acc, jnp.zeros((rows,), x.dtype)


def member_gather(acc, like):
    count = lax.axis_size("member")
    me = lax.axis_index("member")
    out = jnp.zeros((count,) + acc.shape, acc.dtype)
    out = lax.dynamic_update_index_in_dim(out, acc, me, 0)
    for s in range(1, count):
        shift = [(i, (i + s) % count) for i in range(count)]
        got = lax.ppermute(acc, "member", shift)
        out = lax.dynamic_update_index_in_dim(out, got, (me + count - s) % count, 0)
    return out.reshape(count * acc.shape[0], acc.shape[1])[: like.shape[0]]


def member_gather_sum(x):
    count = lax.axis_size("member")
    me = lax.axis_index("member")
    pieces = [None] * count
    pieces[0] = x
    for s in range(1, count):
        shift = [(i, (i + s) % count) for i in range(count)]
        pieces[s] = lax.ppermute(x, "member", shift)
    total = None
    for src in range(count):
        term = pieces[0]
        for s in range(1, count):
            term = jnp.where((me + count - s) % count == src, pieces[s], term)
        total = term if total is None else total + term
    return total


def body(alpha, ensemble, background, measured_values, precision_factor, depth, loc_cols, loc_rows):
    highest = lax.Precision.HIGHEST
    ncol, nfield, nrow = background.shape
    block_cols = ncol // lax.axis_size("member")
    col_start = lax.axis_index("member") * block_cols

    inputs = jnp.concatenate(
        [background, measured_values, precision_factor, depth[:, None, :]], axis=1
    )
    mem = alpha.shape[0]
    cols_b = jnp.broadcast_to(loc_cols, (mem,) + loc_cols.shape)
    rows_b = jnp.broadcast_to(loc_rows, (mem,) + loc_rows.shape)
    def batched(lhs_dim, rhs_dim):
        return (((lhs_dim,), (rhs_dim,)), ((0,), (0,)))

    localized = lax.dot_general(cols_b, alpha, batched(2, 1), precision=highest)
    localized = lax.dot_general(localized, rows_b, batched(2, 2), precision=highest)
    in_before, in_after = shift_rows(
        None, (inputs[:, :, :HALO].transpose(1, 2, 0), inputs[:, :, -HALO:].transpose(1, 2, 0)))
    ext = jnp.concatenate(
        [in_before.transpose(2, 0, 1), inputs, in_after.transpose(2, 0, 1)], axis=2)
    ens = ensemble.astype(jnp.float32)
    partial = jnp.sum(ens * localized[:, :, None, :], axis=0)
    scattered = member_scatter(partial.transpose(1, 0, 2).reshape(nfield * ncol, nrow))
    scattered, partial, ext = lax.optimization_barrier((scattered, partial, ext))
    p_before, p_after = shift_rows(
        None, (partial[:, :, :HALO].transpose(1, 2, 0), partial[:, :, -HALO:].transpose(1, 2, 0)))
    halo = jnp.concatenate([p_before, p_after], axis=1)
    summed = member_gather(*scattered)
    incr_main = summed.reshape(nfield, ncol, nrow)
    incr_halo = member_gather_sum(halo).transpose(0, 2, 1)
    incr = jnp.concatenate(
        [incr_halo[:, :, :HALO], incr_main, incr_halo[:, :, HALO:]], axis=2
    )

    state = [ext[:, i] + incr[i] for i in range(nfield)]
    meas = [ext[:, nfield + i] for i in range(nfield)]
    prec = [ext[:, 2 * nfield + i] for i in range(nfield)]
    dep = ext[:, 3 * nfield]
    pred, adj = dynamics(*state, dep, prec, meas)

    inner = slice(HALO, HALO + nrow)
    pred = jnp.stack([f[:, inner] for f in pred], axis=1)
    predicted_final = lax.dynamic_slice_in_dim(pred, col_start, block_cols, 0)
    adj = jnp.stack([f[:, inner] for f in adj], axis=1)
    projected = jnp.sum(ens * adj[None], axis=2)
    rows_done = lax.dot_general(projected, rows_b, batched(2, 1), precision=highest)
    cost_derivative = alpha + lax.dot_general(cols_b, rows_done, batched(1, 1), precision=highest)
    return (cost_derivative, predicted_final)


def solution(mesh):
    return jax.shard_map(
        body,
        mesh=mesh,
        in_specs=(
            P("member", None, "tile"),
            P("member", None, None, "tile"),
            P(None, None, "tile"),
            P(None, None, "tile"),
            P(None, None, "tile"),
            P(None, "tile"),
            P(),
            P(),
        ),
        out_specs=(P("member", None, "tile"), P("member", None, "tile")),
        check_vma=False,
    )
```

```python
import jax
import jax.numpy as jnp
from jax import lax
from jax.sharding import PartitionSpec as P

STEPS = 2
COURANT = 0.3
HALO = 4 * STEPS


def shift_rows(x, sides):
    count = lax.axis_size("tile")
    up = [(i, (i + 1) % count) for i in range(count)]
    down = [(j, i) for i, j in up]
    lo, hi = sides
    before = lax.ppermute(hi, "tile", up)
    after = lax.ppermute(lo, "tile", down)
    return before, after


def col_slope(f):
    return 0.5 * (jnp.roll(f, -1, 0) - jnp.roll(f, 1, 0))


def row_slope(f):
    return 0.5 * (jnp.roll(f, -1, 1) - jnp.roll(f, 1, 1))


def dynamics(h, u, v, dep, prec, meas):
    for _ in range(STEPS):
        h = h - COURANT * dep * (col_slope(u) + row_slope(v))
        u = u - COURANT * col_slope(h)
        v = v - COURANT * row_slope(h)
    pred = (h, u, v)
    a, p, q = (prec[i] * (pred[i] - meas[i]) for i in range(3))
    for _ in range(STEPS):
        e = a + COURANT * (col_slope(p) + row_slope(q))
        w = dep * e
        p = p + COURANT * col_slope(w)
        q = q + COURANT * row_slope(w)
        a = e
    return pred, (a, p, q)


def member_scatter(x):
    count = lax.axis_size("member")
    me = lax.axis_index("member")
    rows, lanes = x.shape
    piece = -(-rows // (8 * count)) * 8
    x = jnp.pad(x, ((0, piece * count - rows), (0, 0))).reshape(count, piece, lanes)
    acc = lax.dynamic_index_in_dim(x, me, 0, keepdims=False)
    for s in range(1, count):
        shift = [(i, (i + s) % count) for i in range(count)]
        sent = lax.dynamic_index_in_dim(x, (me + s) % count, 0, keepdims=False)
        acc = acc + lax.ppermute(sent, "member", shift)
    return acc, jnp.zeros((rows,), x.dtype)


def member_gather(acc, like):
    count = lax.axis_size("member")
    me = lax.axis_index("member")
    out = jnp.zeros((count,) + acc.shape, acc.dtype)
    out = lax.dynamic_update_index_in_dim(out, acc, me, 0)
    for s in range(1, count):
        shift = [(i, (i + s) % count) for i in range(count)]
        got = lax.ppermute(acc, "member", shift)
        out = lax.dynamic_update_index_in_dim(out, got, (me + count - s) % count, 0)
    return out.reshape(count * acc.shape[0], acc.shape[1])[: like.shape[0]]


def member_gather_sum(x):
    count = lax.axis_size("member")
    me = lax.axis_index("member")
    pieces = [None] * count
    pieces[0] = x
    for s in range(1, count):
        shift = [(i, (i + s) % count) for i in range(count)]
        pieces[s] = lax.ppermute(x, "member", shift)
    total = None
    for src in range(count):
        term = pieces[0]
        for s in range(1, count):
            term = jnp.where((me + count - s) % count == src, pieces[s], term)
        total = term if total is None else total + term
    return total


def body(alpha, ensemble, background, measured_values, precision_factor, depth, loc_cols, loc_rows):
    highest = lax.Precision.HIGHEST
    ncol, nfield, nrow = background.shape
    block_cols = ncol // lax.axis_size("member")
    col_start = lax.axis_index("member") * block_cols

    mem = alpha.shape[0]
    cols_b = jnp.broadcast_to(loc_cols, (mem,) + loc_cols.shape)
    rows_b = jnp.broadcast_to(loc_rows, (mem,) + loc_rows.shape)

    def batched(lhs_dim, rhs_dim):
        return (((lhs_dim,), (rhs_dim,)), ((0,), (0,)))

    localized = lax.dot_general(cols_b, alpha, batched(2, 1), precision=highest)
    localized = lax.dot_general(localized, rows_b, batched(2, 2), precision=highest)
    ens = ensemble.astype(jnp.float32)
    partial = jnp.sum(ens * localized[:, :, None, :], axis=0)
    scattered = member_scatter(partial.transpose(1, 0, 2).reshape(nfield * ncol, nrow))

    meas = [measured_values[:, i] for i in range(nfield)]
    prec = [precision_factor[:, i] for i in range(nfield)]
    fixed = meas + prec + [depth]

    def edges(planes, part):
        return jnp.stack([p[:, part] for p in planes], axis=1)

    lo, hi = slice(0, HALO), slice(nrow - HALO, nrow)
    scattered, fixed_lo, fixed_hi = lax.optimization_barrier(
        (scattered, edges(fixed, lo), edges(fixed, hi)))
    incr = member_gather(*scattered).reshape(nfield, ncol, nrow)
    state = [background[:, i] + incr[i] for i in range(nfield)]

    before, after = shift_rows(None, (
        jnp.concatenate([edges(state, lo), fixed_lo], axis=1),
        jnp.concatenate([edges(state, hi), fixed_hi], axis=1)))
    planes = state + fixed

    pred, adj = dynamics(*state, depth, prec, meas)

    def strip(pieces):
        s = [jnp.concatenate(p, axis=1) for p in pieces]
        return dynamics(*s[:nfield], s[-1], s[2 * nfield:3 * nfield], s[nfield:2 * nfield])

    first = strip([(before[:, i], p[:, : 2 * HALO]) for i, p in enumerate(planes)])
    last = strip([(p[:, nrow - 2 * HALO:], after[:, i]) for i, p in enumerate(planes)])
    mid = slice(HALO, 2 * HALO)
    inner = slice(HALO, nrow - HALO)

    def assemble(k):
        return jnp.stack([
            jnp.concatenate([first[k][i][:, mid], f[:, inner], last[k][i][:, mid]], axis=1)
            for i, f in enumerate((pred, adj)[k])], axis=1)

    predicted_final = lax.dynamic_slice_in_dim(assemble(0), col_start, block_cols, 0)
    projected = jnp.sum(ens * assemble(1)[None], axis=2)
    rows_done = lax.dot_general(projected, rows_b, batched(2, 1), precision=highest)
    cost_derivative = alpha + lax.dot_general(cols_b, rows_done, batched(1, 1), precision=highest)
    return (cost_derivative, predicted_final)


def solution(mesh):
    return jax.shard_map(
        body,
        mesh=mesh,
        in_specs=(
            P("member", None, "tile"),
            P("member", None, None, "tile"),
            P(None, None, "tile"),
            P(None, None, "tile"),
            P(None, None, "tile"),
            P(None, "tile"),
            P(),
            P(),
        ),
        out_specs=(P("member", None, "tile"), P("member", None, "tile")),
        check_vma=False,
    )
```

```python
import jax
import jax.numpy as jnp
from jax import lax
from jax.sharding import PartitionSpec as P

STEPS = 2
COURANT = 0.3
HALO = 4 * STEPS


def shift_rows(x, sides):
    count = lax.axis_size("tile")
    up = [(i, (i + 1) % count) for i in range(count)]
    down = [(j, i) for i, j in up]
    lo, hi = sides
    before = lax.ppermute(hi, "tile", up)
    after = lax.ppermute(lo, "tile", down)
    return before, after


def slope(f, axis):
    return 0.5 * (jnp.roll(f, -1, axis) - jnp.roll(f, 1, axis))


def dynamics(h, u, v, dep, prec, meas, col=0, row=1):
    for _ in range(STEPS):
        h = h - COURANT * dep * (slope(u, col) + slope(v, row))
        u = u - COURANT * slope(h, col)
        v = v - COURANT * slope(h, row)
    pred = (h, u, v)
    a, p, q = (prec[i] * (pred[i] - meas[i]) for i in range(3))
    for _ in range(STEPS):
        e = a + COURANT * (slope(p, col) + slope(q, row))
        w = dep * e
        p = p + COURANT * slope(w, col)
        q = q + COURANT * slope(w, row)
        a = e
    return pred, (a, p, q)


def member_scatter(x):
    count = lax.axis_size("member")
    me = lax.axis_index("member")
    rows, lanes = x.shape
    piece = -(-rows // (8 * count)) * 8
    x = jnp.pad(x, ((0, piece * count - rows), (0, 0))).reshape(count, piece, lanes)
    acc = lax.dynamic_index_in_dim(x, me, 0, keepdims=False)
    for s in range(1, count):
        shift = [(i, (i + s) % count) for i in range(count)]
        sent = lax.dynamic_index_in_dim(x, (me + s) % count, 0, keepdims=False)
        acc = acc + lax.ppermute(sent, "member", shift)
    return acc, jnp.zeros((rows,), x.dtype)


def member_gather(acc, like):
    count = lax.axis_size("member")
    me = lax.axis_index("member")
    out = jnp.zeros((count,) + acc.shape, acc.dtype)
    out = lax.dynamic_update_index_in_dim(out, acc, me, 0)
    for s in range(1, count):
        shift = [(i, (i + s) % count) for i in range(count)]
        got = lax.ppermute(acc, "member", shift)
        out = lax.dynamic_update_index_in_dim(out, got, (me + count - s) % count, 0)
    return out.reshape(count * acc.shape[0], acc.shape[1])[: like.shape[0]]


def member_gather_sum(x):
    count = lax.axis_size("member")
    me = lax.axis_index("member")
    pieces = [None] * count
    pieces[0] = x
    for s in range(1, count):
        shift = [(i, (i + s) % count) for i in range(count)]
        pieces[s] = lax.ppermute(x, "member", shift)
    total = None
    for src in range(count):
        term = pieces[0]
        for s in range(1, count):
            term = jnp.where((me + count - s) % count == src, pieces[s], term)
        total = term if total is None else total + term
    return total


def body(alpha, ensemble, background, measured_values, precision_factor, depth, loc_cols, loc_rows):
    highest = lax.Precision.HIGHEST
    ncol, nfield, nrow = background.shape
    block_cols = ncol // lax.axis_size("member")
    col_start = lax.axis_index("member") * block_cols

    mem = alpha.shape[0]
    cols_b = jnp.broadcast_to(loc_cols, (mem,) + loc_cols.shape)
    rows_b = jnp.broadcast_to(loc_rows, (mem,) + loc_rows.shape)

    def batched(lhs_dim, rhs_dim):
        return (((lhs_dim,), (rhs_dim,)), ((0,), (0,)))

    localized = lax.dot_general(cols_b, alpha, batched(2, 1), precision=highest)
    localized = lax.dot_general(localized, rows_b, batched(2, 2), precision=highest)
    ens = ensemble.astype(jnp.float32)
    partial = jnp.sum(ens * localized[:, :, None, :], axis=0)
    scattered = member_scatter(partial.transpose(1, 0, 2).reshape(nfield * ncol, nrow))

    meas = [measured_values[:, i] for i in range(nfield)]
    prec = [precision_factor[:, i] for i in range(nfield)]
    fixed = meas + prec + [depth]

    def ends(planes):
        return (jnp.stack([p[:, : 2 * HALO] for p in planes]).transpose(0, 2, 1),
                jnp.stack([p[:, nrow - 2 * HALO:] for p in planes]).transpose(0, 2, 1))

    scattered, fixed_lo, fixed_hi = lax.optimization_barrier((scattered,) + ends(fixed))
    incr = member_gather(*scattered).reshape(nfield, ncol, nrow)
    state = [background[:, i] + incr[i] for i in range(nfield)]
    state_lo, state_hi = ends(state)
    own_lo = jnp.concatenate([state_lo, fixed_lo], axis=0)
    own_hi = jnp.concatenate([state_hi, fixed_hi], axis=0)
    before, after = shift_rows(None, (own_lo[:, :HALO], own_hi[:, HALO:]))

    pred, adj = dynamics(*state, depth, prec, meas)

    def strip(s):
        return dynamics(*s[:nfield], s[-1], s[2 * nfield:3 * nfield], s[nfield:2 * nfield],
                        col=1, row=0)

    first = strip(jnp.concatenate([before, own_lo], axis=1))
    last = strip(jnp.concatenate([own_hi, after], axis=1))
    mid = slice(HALO, 2 * HALO)
    inner = slice(HALO, nrow - HALO)

    def assemble(k):
        lo = jnp.stack([f[mid] for f in first[k]]).transpose(2, 0, 1)
        hi = jnp.stack([f[mid] for f in last[k]]).transpose(2, 0, 1)
        block = jnp.stack([f[:, inner] for f in (pred, adj)[k]], axis=1)
        return jnp.concatenate([lo, block, hi], axis=2)

    predicted_final = lax.dynamic_slice_in_dim(assemble(0), col_start, block_cols, 0)
    projected = jnp.sum(ens * assemble(1)[None], axis=2)
    rows_done = lax.dot_general(projected, rows_b, batched(2, 1), precision=highest)
    cost_derivative = alpha + lax.dot_general(cols_b, rows_done, batched(1, 1), precision=highest)
    return (cost_derivative, predicted_final)


def solution(mesh):
    return jax.shard_map(
        body,
        mesh=mesh,
        in_specs=(
            P("member", None, "tile"),
            P("member", None, None, "tile"),
            P(None, None, "tile"),
            P(None, None, "tile"),
            P(None, None, "tile"),
            P(None, "tile"),
            P(),
            P(),
        ),
        out_specs=(P("member", None, "tile"), P("member", None, "tile")),
        check_vma=False,
    )
```

```python
import jax
import jax.numpy as jnp
from jax import lax
from jax.sharding import PartitionSpec as P

STEPS = 2
COURANT = 0.3
HALO = 4 * STEPS


def shift_rows(x, sides):
    count = lax.axis_size("tile")
    up = [(i, (i + 1) % count) for i in range(count)]
    down = [(j, i) for i, j in up]
    lo, hi = sides
    before = lax.ppermute(hi, "tile", up)
    after = lax.ppermute(lo, "tile", down)
    return before, after


def slope(f, axis):
    return 0.5 * (jnp.roll(f, -1, axis) - jnp.roll(f, 1, axis))


def dynamics(h, u, v, dep, prec, meas, col=0, row=1):
    for _ in range(STEPS):
        h = h - COURANT * dep * (slope(u, col) + slope(v, row))
        u = u - COURANT * slope(h, col)
        v = v - COURANT * slope(h, row)
    pred = (h, u, v)
    a, p, q = (prec[i] * (pred[i] - meas[i]) for i in range(3))
    for _ in range(STEPS):
        e = a + COURANT * (slope(p, col) + slope(q, row))
        w = dep * e
        p = p + COURANT * slope(w, col)
        q = q + COURANT * slope(w, row)
        a = e
    return pred, (a, p, q)


def member_scatter(x):
    count = lax.axis_size("member")
    me = lax.axis_index("member")
    rows, lanes = x.shape
    piece = -(-rows // (8 * count)) * 8
    x = jnp.pad(x, ((0, piece * count - rows), (0, 0))).reshape(count, piece, lanes)
    acc = lax.dynamic_index_in_dim(x, me, 0, keepdims=False)
    for s in range(1, count):
        shift = [(i, (i + s) % count) for i in range(count)]
        sent = lax.dynamic_index_in_dim(x, (me + s) % count, 0, keepdims=False)
        acc = acc + lax.ppermute(sent, "member", shift)
    return acc, jnp.zeros((rows,), x.dtype)


def member_gather(acc, like):
    count = lax.axis_size("member")
    me = lax.axis_index("member")
    out = jnp.zeros((count,) + acc.shape, acc.dtype)
    out = lax.dynamic_update_index_in_dim(out, acc, me, 0)
    for s in range(1, count):
        shift = [(i, (i + s) % count) for i in range(count)]
        got = lax.ppermute(acc, "member", shift)
        out = lax.dynamic_update_index_in_dim(out, got, (me + count - s) % count, 0)
    return out.reshape(count * acc.shape[0], acc.shape[1])[: like.shape[0]]


def member_gather_sum(x):
    count = lax.axis_size("member")
    me = lax.axis_index("member")
    pieces = [None] * count
    pieces[0] = x
    for s in range(1, count):
        shift = [(i, (i + s) % count) for i in range(count)]
        pieces[s] = lax.ppermute(x, "member", shift)
    total = None
    for src in range(count):
        term = pieces[0]
        for s in range(1, count):
            term = jnp.where((me + count - s) % count == src, pieces[s], term)
        total = term if total is None else total + term
    return total


def body(alpha, ensemble, background, measured_values, precision_factor, depth, loc_cols, loc_rows):
    highest = lax.Precision.HIGHEST
    ncol, nfield, nrow = background.shape
    block_cols = ncol // lax.axis_size("member")
    col_start = lax.axis_index("member") * block_cols

    mem = alpha.shape[0]
    cols_b = jnp.broadcast_to(loc_cols, (mem,) + loc_cols.shape)
    rows_b = jnp.broadcast_to(loc_rows, (mem,) + loc_rows.shape)

    def batched(lhs_dim, rhs_dim):
        return (((lhs_dim,), (rhs_dim,)), ((0,), (0,)))

    localized = lax.dot_general(cols_b, alpha, batched(2, 1), precision=highest)
    localized = lax.dot_general(localized, rows_b, batched(2, 2), precision=highest)
    ens = ensemble.astype(jnp.float32)
    partial = jnp.sum(ens * localized[:, :, None, :], axis=0)
    scattered = member_scatter(partial.transpose(1, 0, 2).reshape(nfield * ncol, nrow))

    meas = [measured_values[:, i] for i in range(nfield)]
    prec = [precision_factor[:, i] for i in range(nfield)]
    fixed = meas + prec + [depth]

    picked = jnp.concatenate([jnp.arange(2 * HALO), jnp.arange(nrow - 2 * HALO, nrow)])
    select = (picked[:, None] == jnp.arange(nrow)[None, :]).astype(jnp.float32)

    def ends(planes):
        cut = lax.dot_general(select, jnp.stack(planes), (((1,), (2,)), ((), ())),
                              precision=highest).transpose(1, 0, 2)
        return cut[:, : 2 * HALO], cut[:, 2 * HALO:]

    scattered, fixed_lo, fixed_hi = lax.optimization_barrier((scattered,) + ends(fixed))
    incr = member_gather(*scattered).reshape(nfield, ncol, nrow)
    state = [background[:, i] + incr[i] for i in range(nfield)]
    state_lo, state_hi = ends(state)
    own_lo = jnp.concatenate([state_lo, fixed_lo], axis=0)
    own_hi = jnp.concatenate([state_hi, fixed_hi], axis=0)
    before, after = shift_rows(None, (own_lo[:, :HALO], own_hi[:, HALO:]))

    pred, adj = dynamics(*state, depth, prec, meas)

    def strip(s):
        return dynamics(*s[:nfield], s[-1], s[2 * nfield:3 * nfield], s[nfield:2 * nfield],
                        col=1, row=0)

    first = strip(jnp.concatenate([before, own_lo], axis=1))
    last = strip(jnp.concatenate([own_hi, after], axis=1))
    mid = slice(HALO, 2 * HALO)

    placed = jnp.concatenate([jnp.arange(HALO), jnp.arange(nrow - HALO, nrow)])
    place = (placed[:, None] == jnp.arange(nrow)[None, :]).astype(jnp.float32)
    at_edge = (jnp.arange(nrow) < HALO) | (jnp.arange(nrow) >= nrow - HALO)

    def assemble(k):
        rows = jnp.stack([jnp.concatenate([f[mid], g[mid]], axis=0)
                          for f, g in zip(first[k], last[k])])
        edge = lax.dot_general(rows, place, (((1,), (0,)), ((), ())), precision=highest)
        return jnp.stack([jnp.where(at_edge, edge[i], f) for i, f in enumerate((pred, adj)[k])],
                         axis=1)

    predicted_final = lax.dynamic_slice_in_dim(assemble(0), col_start, block_cols, 0)
    projected = jnp.sum(ens * assemble(1)[None], axis=2)
    rows_done = lax.dot_general(projected, rows_b, batched(2, 1), precision=highest)
    cost_derivative = alpha + lax.dot_general(cols_b, rows_done, batched(1, 1), precision=highest)
    return (cost_derivative, predicted_final)


def solution(mesh):
    return jax.shard_map(
        body,
        mesh=mesh,
        in_specs=(
            P("member", None, "tile"),
            P("member", None, None, "tile"),
            P(None, None, "tile"),
            P(None, None, "tile"),
            P(None, None, "tile"),
            P(None, "tile"),
            P(),
            P(),
        ),
        out_specs=(P("member", None, "tile"), P("member", None, "tile")),
        check_vma=False,
    )
```

```python
import jax
import jax.numpy as jnp
from jax import lax
from jax.experimental import pallas as pl
from jax.experimental.pallas import tpu as pltpu
from jax.sharding import PartitionSpec as P

STEPS = 2
COURANT = 0.3
HALO = 4 * STEPS


def shift_rows(x, sides):
    count = lax.axis_size("tile")
    up = [(i, (i + 1) % count) for i in range(count)]
    down = [(j, i) for i, j in up]
    lo, hi = sides
    before = lax.ppermute(hi, "tile", up)
    after = lax.ppermute(lo, "tile", down)
    return before, after


def jnp_slope(f, axis):
    return 0.5 * (jnp.roll(f, -1, axis) - jnp.roll(f, 1, axis))


def kernel_slope(f, axis):
    return 0.5 * (pltpu.roll(f, f.shape[axis] - 1, axis) - pltpu.roll(f, 1, axis))


def dynamics(h, u, v, dep, prec, meas, col=0, row=1, slope=jnp_slope):
    for _ in range(STEPS):
        h = h - COURANT * dep * (slope(u, col) + slope(v, row))
        u = u - COURANT * slope(h, col)
        v = v - COURANT * slope(h, row)
    pred = (h, u, v)
    a, p, q = (prec[i] * (pred[i] - meas[i]) for i in range(3))
    for _ in range(STEPS):
        e = a + COURANT * (slope(p, col) + slope(q, row))
        w = dep * e
        p = p + COURANT * slope(w, col)
        q = q + COURANT * slope(w, row)
        a = e
    return pred, (a, p, q)


def block_kernel(state_ref, meas_ref, prec_ref, dep_ref, pred_ref, adj_ref):
    count = state_ref.shape[0]
    pred, adj = dynamics(*(state_ref[i] for i in range(count)), dep_ref[...],
                         [prec_ref[i] for i in range(count)], [meas_ref[i] for i in range(count)],
                         slope=kernel_slope)
    for i in range(count):
        pred_ref[i] = pred[i]
        adj_ref[i] = adj[i]


def block_dynamics(state, meas, prec, dep):
    vmem = pl.BlockSpec(memory_space=pltpu.VMEM)
    out = jax.ShapeDtypeStruct(state.shape, state.dtype)
    return pl.pallas_call(
        block_kernel,
        out_shape=(out, out),
        in_specs=[vmem] * 4,
        out_specs=(vmem, vmem),
        cost_estimate=pl.CostEstimate(
            flops=120 * state.size, transcendentals=0, bytes_accessed=4 * (6 * state.size + dep.size)),
    )(state, meas, prec, dep)


def member_scatter(x):
    count = lax.axis_size("member")
    me = lax.axis_index("member")
    rows, lanes = x.shape
    piece = -(-rows // (8 * count)) * 8
    x = jnp.pad(x, ((0, piece * count - rows), (0, 0))).reshape(count, piece, lanes)
    acc = lax.dynamic_index_in_dim(x, me, 0, keepdims=False)
    for s in range(1, count):
        shift = [(i, (i + s) % count) for i in range(count)]
        sent = lax.dynamic_index_in_dim(x, (me + s) % count, 0, keepdims=False)
        acc = acc + lax.ppermute(sent, "member", shift)
    return acc, jnp.zeros((rows,), x.dtype)


def member_gather(acc, like):
    count = lax.axis_size("member")
    me = lax.axis_index("member")
    out = jnp.zeros((count,) + acc.shape, acc.dtype)
    out = lax.dynamic_update_index_in_dim(out, acc, me, 0)
    for s in range(1, count):
        shift = [(i, (i + s) % count) for i in range(count)]
        got = lax.ppermute(acc, "member", shift)
        out = lax.dynamic_update_index_in_dim(out, got, (me + count - s) % count, 0)
    return out.reshape(count * acc.shape[0], acc.shape[1])[: like.shape[0]]


def member_gather_sum(x):
    count = lax.axis_size("member")
    me = lax.axis_index("member")
    pieces = [None] * count
    pieces[0] = x
    for s in range(1, count):
        shift = [(i, (i + s) % count) for i in range(count)]
        pieces[s] = lax.ppermute(x, "member", shift)
    total = None
    for src in range(count):
        term = pieces[0]
        for s in range(1, count):
            term = jnp.where((me + count - s) % count == src, pieces[s], term)
        total = term if total is None else total + term
    return total


def body(alpha, ensemble, background, measured_values, precision_factor, depth, loc_cols, loc_rows):
    highest = lax.Precision.HIGHEST
    ncol, nfield, nrow = background.shape
    block_cols = ncol // lax.axis_size("member")
    col_start = lax.axis_index("member") * block_cols

    mem = alpha.shape[0]
    cols_b = jnp.broadcast_to(loc_cols, (mem,) + loc_cols.shape)
    rows_b = jnp.broadcast_to(loc_rows, (mem,) + loc_rows.shape)

    def batched(lhs_dim, rhs_dim):
        return (((lhs_dim,), (rhs_dim,)), ((0,), (0,)))

    localized = lax.dot_general(cols_b, alpha, batched(2, 1), precision=highest)
    localized = lax.dot_general(localized, rows_b, batched(2, 2), precision=highest)
    ens = ensemble.astype(jnp.float32)
    partial = jnp.sum(ens * localized[:, :, None, :], axis=0)
    scattered = member_scatter(partial.transpose(1, 0, 2).reshape(nfield * ncol, nrow))

    meas = [measured_values[:, i] for i in range(nfield)]
    prec = [precision_factor[:, i] for i in range(nfield)]
    fixed = meas + prec + [depth]

    picked = jnp.concatenate([jnp.arange(2 * HALO), jnp.arange(nrow - 2 * HALO, nrow)])
    select = (picked[:, None] == jnp.arange(nrow)[None, :]).astype(jnp.float32)

    def ends(planes):
        cut = lax.dot_general(select, jnp.stack(planes), (((1,), (2,)), ((), ())),
                              precision=highest).transpose(1, 0, 2)
        return cut[:, : 2 * HALO], cut[:, 2 * HALO:]

    scattered, fixed_lo, fixed_hi = lax.optimization_barrier((scattered,) + ends(fixed))
    incr = member_gather(*scattered).reshape(nfield, ncol, nrow)
    state = [background[:, i] + incr[i] for i in range(nfield)]
    state_lo, state_hi = ends(state)
    own_lo = jnp.concatenate([state_lo, fixed_lo], axis=0)
    own_hi = jnp.concatenate([state_hi, fixed_hi], axis=0)
    before, after = shift_rows(None, (own_lo[:, :HALO], own_hi[:, HALO:]))

    pred, adj = block_dynamics(jnp.stack(state), measured_values.transpose(1, 0, 2),
                               precision_factor.transpose(1, 0, 2), depth)

    def strip(s):
        return dynamics(*s[:nfield], s[-1], s[2 * nfield:3 * nfield], s[nfield:2 * nfield],
                        col=1, row=0)

    first = strip(jnp.concatenate([before, own_lo], axis=1))
    last = strip(jnp.concatenate([own_hi, after], axis=1))
    mid = slice(HALO, 2 * HALO)

    placed = jnp.concatenate([jnp.arange(HALO), jnp.arange(nrow - HALO, nrow)])
    place = (placed[:, None] == jnp.arange(nrow)[None, :]).astype(jnp.float32)
    at_edge = (jnp.arange(nrow) < HALO) | (jnp.arange(nrow) >= nrow - HALO)

    def assemble(k):
        rows = jnp.stack([jnp.concatenate([f[mid], g[mid]], axis=0)
                          for f, g in zip(first[k], last[k])])
        edge = lax.dot_general(rows, place, (((1,), (0,)), ((), ())), precision=highest)
        return jnp.stack([jnp.where(at_edge, edge[i], f) for i, f in enumerate((pred, adj)[k])],
                         axis=1)

    predicted_final = lax.dynamic_slice_in_dim(assemble(0), col_start, block_cols, 0)
    projected = jnp.sum(ens * assemble(1)[None], axis=2)
    rows_done = lax.dot_general(projected, rows_b, batched(2, 1), precision=highest)
    cost_derivative = alpha + lax.dot_general(cols_b, rows_done, batched(1, 1), precision=highest)
    return (cost_derivative, predicted_final)


def solution(mesh):
    return jax.shard_map(
        body,
        mesh=mesh,
        in_specs=(
            P("member", None, "tile"),
            P("member", None, None, "tile"),
            P(None, None, "tile"),
            P(None, None, "tile"),
            P(None, None, "tile"),
            P(None, "tile"),
            P(),
            P(),
        ),
        out_specs=(P("member", None, "tile"), P("member", None, "tile")),
        check_vma=False,
    )
```

```python
import jax
import jax.numpy as jnp
from jax import lax
from jax.experimental import pallas as pl
from jax.experimental.pallas import tpu as pltpu
from jax.sharding import PartitionSpec as P

STEPS = 2
COURANT = 0.3
HALO = 4 * STEPS


def shift_rows(x, sides):
    count = lax.axis_size("tile")
    up = [(i, (i + 1) % count) for i in range(count)]
    down = [(j, i) for i, j in up]
    lo, hi = sides
    before = lax.ppermute(hi, "tile", up)
    after = lax.ppermute(lo, "tile", down)
    return before, after


def jnp_slope(f, axis):
    return 0.5 * (jnp.roll(f, -1, axis) - jnp.roll(f, 1, axis))


def kernel_slope(f, axis):
    return 0.5 * (pltpu.roll(f, f.shape[axis] - 1, axis) - pltpu.roll(f, 1, axis))


def dynamics(h, u, v, dep, prec, meas, col=0, row=1, slope=jnp_slope):
    for _ in range(STEPS):
        h = h - COURANT * dep * (slope(u, col) + slope(v, row))
        u = u - COURANT * slope(h, col)
        v = v - COURANT * slope(h, row)
    pred = (h, u, v)
    a, p, q = (prec[i] * (pred[i] - meas[i]) for i in range(3))
    for _ in range(STEPS):
        e = a + COURANT * (slope(p, col) + slope(q, row))
        w = dep * e
        p = p + COURANT * slope(w, col)
        q = q + COURANT * slope(w, row)
        a = e
    return pred, (a, p, q)


def block_kernel(back_ref, incr_ref, meas_ref, prec_ref, dep_ref, pred_ref, adj_ref):
    count = back_ref.shape[0]
    pred, adj = dynamics(*(back_ref[i] + incr_ref[i] for i in range(count)), dep_ref[...],
                         [prec_ref[i] for i in range(count)], [meas_ref[i] for i in range(count)],
                         slope=kernel_slope)
    for i in range(count):
        pred_ref[i] = pred[i]
        adj_ref[i] = adj[i]


def block_dynamics(back, incr, meas, prec, dep):
    vmem = pl.BlockSpec(memory_space=pltpu.VMEM)
    out = jax.ShapeDtypeStruct(back.shape, back.dtype)
    return pl.pallas_call(
        block_kernel,
        out_shape=(out, out),
        in_specs=[vmem] * 5,
        out_specs=(vmem, vmem),
        cost_estimate=pl.CostEstimate(
            flops=120 * back.size, transcendentals=0, bytes_accessed=4 * (7 * back.size + dep.size)),
    )(back, incr, meas, prec, dep)


def member_scatter(x):
    count = lax.axis_size("member")
    me = lax.axis_index("member")
    rows, lanes = x.shape
    piece = -(-rows // (8 * count)) * 8
    x = jnp.pad(x, ((0, piece * count - rows), (0, 0))).reshape(count, piece, lanes)
    acc = lax.dynamic_index_in_dim(x, me, 0, keepdims=False)
    for s in range(1, count):
        shift = [(i, (i + s) % count) for i in range(count)]
        sent = lax.dynamic_index_in_dim(x, (me + s) % count, 0, keepdims=False)
        acc = acc + lax.ppermute(sent, "member", shift)
    return acc, jnp.zeros((rows,), x.dtype)


def member_gather(acc, like):
    count = lax.axis_size("member")
    me = lax.axis_index("member")
    out = jnp.zeros((count,) + acc.shape, acc.dtype)
    out = lax.dynamic_update_index_in_dim(out, acc, me, 0)
    for s in range(1, count):
        shift = [(i, (i + s) % count) for i in range(count)]
        got = lax.ppermute(acc, "member", shift)
        out = lax.dynamic_update_index_in_dim(out, got, (me + count - s) % count, 0)
    return out.reshape(count * acc.shape[0], acc.shape[1])[: like.shape[0]]


def member_gather_sum(x):
    count = lax.axis_size("member")
    me = lax.axis_index("member")
    pieces = [None] * count
    pieces[0] = x
    for s in range(1, count):
        shift = [(i, (i + s) % count) for i in range(count)]
        pieces[s] = lax.ppermute(x, "member", shift)
    total = None
    for src in range(count):
        term = pieces[0]
        for s in range(1, count):
            term = jnp.where((me + count - s) % count == src, pieces[s], term)
        total = term if total is None else total + term
    return total


def body(alpha, ensemble, background, measured_values, precision_factor, depth, loc_cols, loc_rows):
    highest = lax.Precision.HIGHEST
    ncol, nfield, nrow = background.shape
    block_cols = ncol // lax.axis_size("member")
    col_start = lax.axis_index("member") * block_cols

    mem = alpha.shape[0]
    cols_b = jnp.broadcast_to(loc_cols, (mem,) + loc_cols.shape)
    rows_b = jnp.broadcast_to(loc_rows, (mem,) + loc_rows.shape)

    def batched(lhs_dim, rhs_dim):
        return (((lhs_dim,), (rhs_dim,)), ((0,), (0,)))

    localized = lax.dot_general(cols_b, alpha, batched(2, 1), precision=highest)
    localized = lax.dot_general(localized, rows_b, batched(2, 2), precision=highest)
    ens = ensemble.astype(jnp.float32)
    partial = jnp.sum(ens * localized[:, :, None, :], axis=0)
    scattered = member_scatter(partial.transpose(1, 0, 2).reshape(nfield * ncol, nrow))

    meas = [measured_values[:, i] for i in range(nfield)]
    prec = [precision_factor[:, i] for i in range(nfield)]
    fixed = meas + prec + [depth]

    picked = jnp.concatenate([jnp.arange(2 * HALO), jnp.arange(nrow - 2 * HALO, nrow)])
    select = (picked[:, None] == jnp.arange(nrow)[None, :]).astype(jnp.float32)

    def ends(planes):
        cut = lax.dot_general(select, jnp.stack(planes), (((1,), (2,)), ((), ())),
                              precision=highest).transpose(1, 0, 2)
        return cut[:, : 2 * HALO], cut[:, 2 * HALO:]

    scattered, fixed_lo, fixed_hi = lax.optimization_barrier((scattered,) + ends(fixed))
    incr = member_gather(*scattered).reshape(nfield, ncol, nrow)
    state = [background[:, i] + incr[i] for i in range(nfield)]
    state_lo, state_hi = ends(state)
    own_lo = jnp.concatenate([state_lo, fixed_lo], axis=0)
    own_hi = jnp.concatenate([state_hi, fixed_hi], axis=0)
    before, after = shift_rows(None, (own_lo[:, :HALO], own_hi[:, HALO:]))

    pred, adj = block_dynamics(background.transpose(1, 0, 2), incr, measured_values.transpose(1, 0, 2),
                               precision_factor.transpose(1, 0, 2), depth)

    def strip(s):
        return dynamics(*s[:nfield], s[-1], s[2 * nfield:3 * nfield], s[nfield:2 * nfield],
                        col=1, row=0)

    first = strip(jnp.concatenate([before, own_lo], axis=1))
    last = strip(jnp.concatenate([own_hi, after], axis=1))
    mid = slice(HALO, 2 * HALO)

    placed = jnp.concatenate([jnp.arange(HALO), jnp.arange(nrow - HALO, nrow)])
    place = (placed[:, None] == jnp.arange(nrow)[None, :]).astype(jnp.float32)
    at_edge = (jnp.arange(nrow) < HALO) | (jnp.arange(nrow) >= nrow - HALO)

    def assemble(k):
        rows = jnp.stack([jnp.concatenate([f[mid], g[mid]], axis=0)
                          for f, g in zip(first[k], last[k])])
        edge = lax.dot_general(rows, place, (((1,), (0,)), ((), ())), precision=highest)
        return jnp.stack([jnp.where(at_edge, edge[i], f) for i, f in enumerate((pred, adj)[k])],
                         axis=1)

    predicted_final = lax.dynamic_slice_in_dim(assemble(0), col_start, block_cols, 0)
    projected = jnp.sum(ens * assemble(1)[None], axis=2)
    rows_done = lax.dot_general(projected, rows_b, batched(2, 1), precision=highest)
    cost_derivative = alpha + lax.dot_general(cols_b, rows_done, batched(1, 1), precision=highest)
    return (cost_derivative, predicted_final)


def solution(mesh):
    return jax.shard_map(
        body,
        mesh=mesh,
        in_specs=(
            P("member", None, "tile"),
            P("member", None, None, "tile"),
            P(None, None, "tile"),
            P(None, None, "tile"),
            P(None, None, "tile"),
            P(None, "tile"),
            P(),
            P(),
        ),
        out_specs=(P("member", None, "tile"), P("member", None, "tile")),
        check_vma=False,
    )
```

```python
import jax
import jax.numpy as jnp
from jax import lax
from jax.experimental import pallas as pl
from jax.experimental.pallas import tpu as pltpu
from jax.sharding import PartitionSpec as P

STEPS = 2
COURANT = 0.3
HALO = 4 * STEPS


def shift_rows(x, sides):
    count = lax.axis_size("tile")
    up = [(i, (i + 1) % count) for i in range(count)]
    down = [(j, i) for i, j in up]
    lo, hi = sides
    before = lax.ppermute(hi, "tile", up)
    after = lax.ppermute(lo, "tile", down)
    return before, after


def jnp_slope(f, axis):
    return 0.5 * (jnp.roll(f, -1, axis) - jnp.roll(f, 1, axis))


def kernel_slope(f, axis):
    return 0.5 * (pltpu.roll(f, f.shape[axis] - 1, axis) - pltpu.roll(f, 1, axis))


def dynamics(h, u, v, dep, prec, meas, col=0, row=1, slope=jnp_slope):
    for _ in range(STEPS):
        h = h - COURANT * dep * (slope(u, col) + slope(v, row))
        u = u - COURANT * slope(h, col)
        v = v - COURANT * slope(h, row)
    pred = (h, u, v)
    a, p, q = (prec[i] * (pred[i] - meas[i]) for i in range(3))
    for _ in range(STEPS):
        e = a + COURANT * (slope(p, col) + slope(q, row))
        w = dep * e
        p = p + COURANT * slope(w, col)
        q = q + COURANT * slope(w, row)
        a = e
    return pred, (a, p, q)


def block_kernel(back_ref, incr_ref, meas_ref, prec_ref, dep_ref, pred_ref, adj_ref):
    count = back_ref.shape[0]
    pred, adj = dynamics(*(back_ref[i] + incr_ref[i] for i in range(count)), dep_ref[...],
                         [prec_ref[i] for i in range(count)], [meas_ref[i] for i in range(count)],
                         slope=kernel_slope)
    for i in range(count):
        pred_ref[i] = pred[i]
        adj_ref[i] = adj[i]


def block_dynamics(back, incr, meas, prec, dep):
    vmem = pl.BlockSpec(memory_space=pltpu.VMEM)
    out = jax.ShapeDtypeStruct(back.shape, back.dtype)
    return pl.pallas_call(
        block_kernel,
        out_shape=(out, out),
        in_specs=[vmem] * 5,
        out_specs=(vmem, vmem),
        cost_estimate=pl.CostEstimate(
            flops=120 * back.size, transcendentals=0, bytes_accessed=4 * (7 * back.size + dep.size)),
    )(back, incr, meas, prec, dep)


def strip_kernel(planes_ref, pred_ref, adj_ref):
    count = pred_ref.shape[1]
    for k in range(planes_ref.shape[0]):
        s = [planes_ref[k, i] for i in range(planes_ref.shape[1])]
        pred, adj = dynamics(*s[:count], s[-1], s[2 * count:3 * count], s[count:2 * count],
                             col=1, row=0, slope=kernel_slope)
        for i in range(count):
            pred_ref[k, i] = pred[i]
            adj_ref[k, i] = adj[i]


def strip_dynamics(planes):
    strips, count, rows, cols = planes.shape[0], (planes.shape[1] - 1) // 3, planes.shape[2], planes.shape[3]
    vmem = pl.BlockSpec(memory_space=pltpu.VMEM)
    out = jax.ShapeDtypeStruct((strips, count, rows, cols), planes.dtype)
    pred, adj = pl.pallas_call(
        strip_kernel,
        out_shape=(out, out),
        in_specs=[vmem],
        out_specs=(vmem, vmem),
        cost_estimate=pl.CostEstimate(
            flops=40 * planes.size, transcendentals=0, bytes_accessed=4 * (planes.size + 2 * out.size)),
    )(planes)
    return (pred[0], adj[0]), (pred[1], adj[1])


def member_scatter(x):
    count = lax.axis_size("member")
    me = lax.axis_index("member")
    rows, lanes = x.shape
    piece = -(-rows // (8 * count)) * 8
    x = jnp.pad(x, ((0, piece * count - rows), (0, 0))).reshape(count, piece, lanes)
    acc = lax.dynamic_index_in_dim(x, me, 0, keepdims=False)
    for s in range(1, count):
        shift = [(i, (i + s) % count) for i in range(count)]
        sent = lax.dynamic_index_in_dim(x, (me + s) % count, 0, keepdims=False)
        acc = acc + lax.ppermute(sent, "member", shift)
    return acc, jnp.zeros((rows,), x.dtype)


def member_gather(acc, like):
    count = lax.axis_size("member")
    me = lax.axis_index("member")
    out = jnp.zeros((count,) + acc.shape, acc.dtype)
    out = lax.dynamic_update_index_in_dim(out, acc, me, 0)
    for s in range(1, count):
        shift = [(i, (i + s) % count) for i in range(count)]
        got = lax.ppermute(acc, "member", shift)
        out = lax.dynamic_update_index_in_dim(out, got, (me + count - s) % count, 0)
    return out.reshape(count * acc.shape[0], acc.shape[1])[: like.shape[0]]


def member_gather_sum(x):
    count = lax.axis_size("member")
    me = lax.axis_index("member")
    pieces = [None] * count
    pieces[0] = x
    for s in range(1, count):
        shift = [(i, (i + s) % count) for i in range(count)]
        pieces[s] = lax.ppermute(x, "member", shift)
    total = None
    for src in range(count):
        term = pieces[0]
        for s in range(1, count):
            term = jnp.where((me + count - s) % count == src, pieces[s], term)
        total = term if total is None else total + term
    return total


def body(alpha, ensemble, background, measured_values, precision_factor, depth, loc_cols, loc_rows):
    highest = lax.Precision.HIGHEST
    ncol, nfield, nrow = background.shape
    block_cols = ncol // lax.axis_size("member")
    col_start = lax.axis_index("member") * block_cols

    mem = alpha.shape[0]
    cols_b = jnp.broadcast_to(loc_cols, (mem,) + loc_cols.shape)
    rows_b = jnp.broadcast_to(loc_rows, (mem,) + loc_rows.shape)

    def batched(lhs_dim, rhs_dim):
        return (((lhs_dim,), (rhs_dim,)), ((0,), (0,)))

    localized = lax.dot_general(cols_b, alpha, batched(2, 1), precision=highest)
    localized = lax.dot_general(localized, rows_b, batched(2, 2), precision=highest)
    ens = ensemble.astype(jnp.float32)
    partial = jnp.sum(ens * localized[:, :, None, :], axis=0)
    scattered = member_scatter(partial.transpose(1, 0, 2).reshape(nfield * ncol, nrow))

    meas = [measured_values[:, i] for i in range(nfield)]
    prec = [precision_factor[:, i] for i in range(nfield)]
    fixed = meas + prec + [depth]

    picked = jnp.concatenate([jnp.arange(2 * HALO), jnp.arange(nrow - 2 * HALO, nrow)])
    select = (picked[:, None] == jnp.arange(nrow)[None, :]).astype(jnp.float32)

    def ends(planes):
        cut = lax.dot_general(select, planes, (((1,), (planes.ndim - 1,)), ((), ())),
                              precision=highest)
        cut = cut.transpose(1, 0, 2) if planes.ndim == 3 else cut[None]
        return cut[:, : 2 * HALO], cut[:, 2 * HALO:]

    def fixed_ends():
        parts = [ends(x) for x in (measured_values.transpose(1, 0, 2),
                                   precision_factor.transpose(1, 0, 2), depth)]
        return tuple(jnp.concatenate([p[j] for p in parts], axis=0) for j in range(2))

    scattered, fixed_lo, fixed_hi = lax.optimization_barrier((scattered,) + fixed_ends())
    incr = member_gather(*scattered).reshape(nfield, ncol, nrow)
    state = [background[:, i] + incr[i] for i in range(nfield)]
    state_lo, state_hi = ends(jnp.stack(state))
    own_lo = jnp.concatenate([state_lo, fixed_lo], axis=0)
    own_hi = jnp.concatenate([state_hi, fixed_hi], axis=0)
    before, after = shift_rows(None, (own_lo[:, :HALO], own_hi[:, HALO:]))

    pred, adj = block_dynamics(background.transpose(1, 0, 2), incr, measured_values.transpose(1, 0, 2),
                               precision_factor.transpose(1, 0, 2), depth)

    first, last = strip_dynamics(jnp.stack([jnp.concatenate([before, own_lo], axis=1),
                                            jnp.concatenate([own_hi, after], axis=1)]))
    mid = slice(HALO, 2 * HALO)

    placed = jnp.concatenate([jnp.arange(HALO), jnp.arange(nrow - HALO, nrow)])
    place = (placed[:, None] == jnp.arange(nrow)[None, :]).astype(jnp.float32)
    at_edge = (jnp.arange(nrow) < HALO) | (jnp.arange(nrow) >= nrow - HALO)

    def assemble(k):
        rows = jnp.stack([jnp.concatenate([f[mid], g[mid]], axis=0)
                          for f, g in zip(first[k], last[k])])
        edge = lax.dot_general(rows, place, (((1,), (0,)), ((), ())), precision=highest)
        return jnp.stack([jnp.where(at_edge, edge[i], f) for i, f in enumerate((pred, adj)[k])],
                         axis=1)

    predicted_final = lax.dynamic_slice_in_dim(assemble(0), col_start, block_cols, 0)
    projected = jnp.sum(ens * assemble(1)[None], axis=2)
    rows_done = lax.dot_general(projected, rows_b, batched(2, 1), precision=highest)
    cost_derivative = alpha + lax.dot_general(cols_b, rows_done, batched(1, 1), precision=highest)
    return (cost_derivative, predicted_final)


def solution(mesh):
    return jax.shard_map(
        body,
        mesh=mesh,
        in_specs=(
            P("member", None, "tile"),
            P("member", None, None, "tile"),
            P(None, None, "tile"),
            P(None, None, "tile"),
            P(None, None, "tile"),
            P(None, "tile"),
            P(),
            P(),
        ),
        out_specs=(P("member", None, "tile"), P("member", None, "tile")),
        check_vma=False,
    )
```

```python
import jax
import jax.numpy as jnp
from jax import lax
from jax.experimental import pallas as pl
from jax.experimental.pallas import tpu as pltpu
from jax.sharding import PartitionSpec as P

STEPS = 2
COURANT = 0.3
HALO = 4 * STEPS


def shift_rows(x, sides):
    count = lax.axis_size("tile")
    up = [(i, (i + 1) % count) for i in range(count)]
    down = [(j, i) for i, j in up]
    lo, hi = sides
    before = lax.ppermute(hi, "tile", up)
    after = lax.ppermute(lo, "tile", down)
    return before, after


def jnp_slope(f, axis):
    return 0.5 * (jnp.roll(f, -1, axis) - jnp.roll(f, 1, axis))


def kernel_slope(f, axis):
    return 0.5 * (pltpu.roll(f, f.shape[axis] - 1, axis) - pltpu.roll(f, 1, axis))


def dynamics(h, u, v, dep, prec, meas, col=0, row=1, slope=jnp_slope):
    for _ in range(STEPS):
        h = h - COURANT * dep * (slope(u, col) + slope(v, row))
        u = u - COURANT * slope(h, col)
        v = v - COURANT * slope(h, row)
    pred = (h, u, v)
    a, p, q = (prec[i] * (pred[i] - meas[i]) for i in range(3))
    for _ in range(STEPS):
        e = a + COURANT * (slope(p, col) + slope(q, row))
        w = dep * e
        p = p + COURANT * slope(w, col)
        q = q + COURANT * slope(w, row)
        a = e
    return pred, (a, p, q)


def block_kernel(back_ref, incr_ref, meas_ref, prec_ref, dep_ref, pred_ref, adj_ref):
    count = back_ref.shape[0]
    pred, adj = dynamics(*(back_ref[i] + incr_ref[i] for i in range(count)), dep_ref[...],
                         [prec_ref[i] for i in range(count)], [meas_ref[i] for i in range(count)],
                         slope=kernel_slope)
    for i in range(count):
        pred_ref[i] = pred[i]
        adj_ref[i] = adj[i]


def block_dynamics(back, incr, meas, prec, dep):
    vmem = pl.BlockSpec(memory_space=pltpu.VMEM)
    out = jax.ShapeDtypeStruct(back.shape, back.dtype)
    return pl.pallas_call(
        block_kernel,
        out_shape=(out, out),
        in_specs=[vmem] * 5,
        out_specs=(vmem, vmem),
        cost_estimate=pl.CostEstimate(
            flops=120 * back.size, transcendentals=0, bytes_accessed=4 * (7 * back.size + dep.size)),
    )(back, incr, meas, prec, dep)


def strip_kernel(before_ref, own_lo_ref, own_hi_ref, after_ref, pred_ref, adj_ref):
    count = pred_ref.shape[0]
    halo = before_ref.shape[1]
    planes = before_ref.shape[0]
    for k, (top, bottom) in enumerate(((before_ref, own_lo_ref), (own_hi_ref, after_ref))):
        s = [jnp.concatenate([top[i], bottom[i]], axis=0) for i in range(planes)]
        pred, adj = dynamics(*s[:count], s[-1], s[2 * count:3 * count], s[count:2 * count],
                             col=1, row=0, slope=kernel_slope)
        for i in range(count):
            pred_ref[i, k * halo:(k + 1) * halo] = pred[i][halo:2 * halo]
            adj_ref[i, k * halo:(k + 1) * halo] = adj[i][halo:2 * halo]


def strip_dynamics(before, own_lo, own_hi, after):
    count = (before.shape[0] - 1) // 3
    vmem = pl.BlockSpec(memory_space=pltpu.VMEM)
    out = jax.ShapeDtypeStruct((count, 2 * before.shape[1], before.shape[2]), before.dtype)
    size = 2 * (before.size + own_lo.size)
    return pl.pallas_call(
        strip_kernel,
        out_shape=(out, out),
        in_specs=[vmem] * 4,
        out_specs=(vmem, vmem),
        cost_estimate=pl.CostEstimate(
            flops=40 * size, transcendentals=0, bytes_accessed=4 * (size + 2 * out.size)),
    )(before, own_lo, own_hi, after)


def member_scatter(x):
    count = lax.axis_size("member")
    me = lax.axis_index("member")
    rows, lanes = x.shape
    piece = -(-rows // (8 * count)) * 8
    x = jnp.pad(x, ((0, piece * count - rows), (0, 0))).reshape(count, piece, lanes)
    acc = lax.dynamic_index_in_dim(x, me, 0, keepdims=False)
    for s in range(1, count):
        shift = [(i, (i + s) % count) for i in range(count)]
        sent = lax.dynamic_index_in_dim(x, (me + s) % count, 0, keepdims=False)
        acc = acc + lax.ppermute(sent, "member", shift)
    return acc, jnp.zeros((rows,), x.dtype)


def member_gather(acc, like):
    count = lax.axis_size("member")
    me = lax.axis_index("member")
    out = jnp.zeros((count,) + acc.shape, acc.dtype)
    out = lax.dynamic_update_index_in_dim(out, acc, me, 0)
    for s in range(1, count):
        shift = [(i, (i + s) % count) for i in range(count)]
        got = lax.ppermute(acc, "member", shift)
        out = lax.dynamic_update_index_in_dim(out, got, (me + count - s) % count, 0)
    return out.reshape(count * acc.shape[0], acc.shape[1])[: like.shape[0]]


def member_gather_sum(x):
    count = lax.axis_size("member")
    me = lax.axis_index("member")
    pieces = [None] * count
    pieces[0] = x
    for s in range(1, count):
        shift = [(i, (i + s) % count) for i in range(count)]
        pieces[s] = lax.ppermute(x, "member", shift)
    total = None
    for src in range(count):
        term = pieces[0]
        for s in range(1, count):
            term = jnp.where((me + count - s) % count == src, pieces[s], term)
        total = term if total is None else total + term
    return total


def body(alpha, ensemble, background, measured_values, precision_factor, depth, loc_cols, loc_rows):
    highest = lax.Precision.HIGHEST
    ncol, nfield, nrow = background.shape
    block_cols = ncol // lax.axis_size("member")
    col_start = lax.axis_index("member") * block_cols

    mem = alpha.shape[0]
    cols_b = jnp.broadcast_to(loc_cols, (mem,) + loc_cols.shape)
    rows_b = jnp.broadcast_to(loc_rows, (mem,) + loc_rows.shape)

    def batched(lhs_dim, rhs_dim):
        return (((lhs_dim,), (rhs_dim,)), ((0,), (0,)))

    localized = lax.dot_general(cols_b, alpha, batched(2, 1), precision=highest)
    localized = lax.dot_general(localized, rows_b, batched(2, 2), precision=highest)
    ens = ensemble.astype(jnp.float32)
    partial = jnp.sum(ens * localized[:, :, None, :], axis=0)
    scattered = member_scatter(partial.transpose(1, 0, 2).reshape(nfield * ncol, nrow))

    meas = [measured_values[:, i] for i in range(nfield)]
    prec = [precision_factor[:, i] for i in range(nfield)]
    fixed = meas + prec + [depth]

    picked = jnp.concatenate([jnp.arange(2 * HALO), jnp.arange(nrow - 2 * HALO, nrow)])
    select = (picked[:, None] == jnp.arange(nrow)[None, :]).astype(jnp.float32)

    def ends(planes):
        cut = lax.dot_general(select, jnp.stack(planes), (((1,), (2,)), ((), ())),
                              precision=highest).transpose(1, 0, 2)
        return cut[:, : 2 * HALO], cut[:, 2 * HALO:]

    scattered, fixed_lo, fixed_hi = lax.optimization_barrier((scattered,) + ends(fixed))
    incr = member_gather(*scattered).reshape(nfield, ncol, nrow)
    state = [background[:, i] + incr[i] for i in range(nfield)]
    state_lo, state_hi = ends(state)
    own_lo = jnp.concatenate([state_lo, fixed_lo], axis=0)
    own_hi = jnp.concatenate([state_hi, fixed_hi], axis=0)
    before, after = shift_rows(None, (own_lo[:, :HALO], own_hi[:, HALO:]))

    pred, adj = block_dynamics(background.transpose(1, 0, 2), incr, measured_values.transpose(1, 0, 2),
                               precision_factor.transpose(1, 0, 2), depth)

    edge_rows = strip_dynamics(before, own_lo, own_hi, after)

    placed = jnp.concatenate([jnp.arange(HALO), jnp.arange(nrow - HALO, nrow)])
    place = (placed[:, None] == jnp.arange(nrow)[None, :]).astype(jnp.float32)
    at_edge = (jnp.arange(nrow) < HALO) | (jnp.arange(nrow) >= nrow - HALO)

    def assemble(k):
        edge = lax.dot_general(edge_rows[k], place, (((1,), (0,)), ((), ())), precision=highest)
        return jnp.stack([jnp.where(at_edge, edge[i], f) for i, f in enumerate((pred, adj)[k])],
                         axis=1)

    predicted_final = lax.dynamic_slice_in_dim(assemble(0), col_start, block_cols, 0)
    projected = jnp.sum(ens * assemble(1)[None], axis=2)
    rows_done = lax.dot_general(projected, rows_b, batched(2, 1), precision=highest)
    cost_derivative = alpha + lax.dot_general(cols_b, rows_done, batched(1, 1), precision=highest)
    return (cost_derivative, predicted_final)


def solution(mesh):
    return jax.shard_map(
        body,
        mesh=mesh,
        in_specs=(
            P("member", None, "tile"),
            P("member", None, None, "tile"),
            P(None, None, "tile"),
            P(None, None, "tile"),
            P(None, None, "tile"),
            P(None, "tile"),
            P(),
            P(),
        ),
        out_specs=(P("member", None, "tile"), P("member", None, "tile")),
        check_vma=False,
    )
```

```python
import jax
import jax.numpy as jnp
from jax import lax
from jax.experimental import pallas as pl
from jax.experimental.pallas import tpu as pltpu
from jax.sharding import PartitionSpec as P

STEPS = 2
COURANT = 0.3
HALO = 4 * STEPS


def shift_rows(x, sides):
    count = lax.axis_size("tile")
    up = [(i, (i + 1) % count) for i in range(count)]
    down = [(j, i) for i, j in up]
    lo, hi = sides
    before = lax.ppermute(hi, "tile", up)
    after = lax.ppermute(lo, "tile", down)
    return before, after


def jnp_slope(f, axis):
    return 0.5 * (jnp.roll(f, -1, axis) - jnp.roll(f, 1, axis))


def kernel_slope(f, axis):
    return 0.5 * (pltpu.roll(f, f.shape[axis] - 1, axis) - pltpu.roll(f, 1, axis))


def dynamics(h, u, v, dep, prec, meas, col=0, row=1, slope=jnp_slope):
    for _ in range(STEPS):
        h = h - COURANT * dep * (slope(u, col) + slope(v, row))
        u = u - COURANT * slope(h, col)
        v = v - COURANT * slope(h, row)
    pred = (h, u, v)
    a, p, q = (prec[i] * (pred[i] - meas[i]) for i in range(3))
    for _ in range(STEPS):
        e = a + COURANT * (slope(p, col) + slope(q, row))
        w = dep * e
        p = p + COURANT * slope(w, col)
        q = q + COURANT * slope(w, row)
        a = e
    return pred, (a, p, q)


def block_kernel(back_ref, incr_ref, meas_ref, prec_ref, dep_ref, pred_ref, adj_ref):
    count = back_ref.shape[0]
    pred, adj = dynamics(*(back_ref[i] + incr_ref[i] for i in range(count)), dep_ref[...],
                         [prec_ref[i] for i in range(count)], [meas_ref[i] for i in range(count)],
                         slope=kernel_slope)
    for i in range(count):
        pred_ref[i] = pred[i]
        adj_ref[i] = adj[i]


def block_dynamics(back, incr, meas, prec, dep):
    vmem = pl.BlockSpec(memory_space=pltpu.VMEM)
    out = jax.ShapeDtypeStruct(back.shape, back.dtype)
    return pl.pallas_call(
        block_kernel,
        out_shape=(out, out),
        in_specs=[vmem] * 5,
        out_specs=(vmem, vmem),
        cost_estimate=pl.CostEstimate(
            flops=120 * back.size, transcendentals=0, bytes_accessed=4 * (7 * back.size + dep.size)),
    )(back, incr, meas, prec, dep)


def member_scatter(x):
    count = lax.axis_size("member")
    me = lax.axis_index("member")
    rows, lanes = x.shape
    piece = -(-rows // (8 * count)) * 8
    x = jnp.pad(x, ((0, piece * count - rows), (0, 0))).reshape(count, piece, lanes)
    acc = lax.dynamic_index_in_dim(x, me, 0, keepdims=False)
    for s in range(1, count):
        shift = [(i, (i + s) % count) for i in range(count)]
        sent = lax.dynamic_index_in_dim(x, (me + s) % count, 0, keepdims=False)
        acc = acc + lax.ppermute(sent, "member", shift)
    return acc, jnp.zeros((rows,), x.dtype)


def member_gather(acc, like):
    count = lax.axis_size("member")
    me = lax.axis_index("member")
    out = jnp.zeros((count,) + acc.shape, acc.dtype)
    out = lax.dynamic_update_index_in_dim(out, acc, me, 0)
    for s in range(1, count):
        shift = [(i, (i + s) % count) for i in range(count)]
        got = lax.ppermute(acc, "member", shift)
        out = lax.dynamic_update_index_in_dim(out, got, (me + count - s) % count, 0)
    return out.reshape(count * acc.shape[0], acc.shape[1])[: like.shape[0]]


def member_gather_sum(x):
    count = lax.axis_size("member")
    me = lax.axis_index("member")
    pieces = [None] * count
    pieces[0] = x
    for s in range(1, count):
        shift = [(i, (i + s) % count) for i in range(count)]
        pieces[s] = lax.ppermute(x, "member", shift)
    total = None
    for src in range(count):
        term = pieces[0]
        for s in range(1, count):
            term = jnp.where((me + count - s) % count == src, pieces[s], term)
        total = term if total is None else total + term
    return total


def body(alpha, ensemble, background, measured_values, precision_factor, depth, loc_cols, loc_rows):
    highest = lax.Precision.HIGHEST
    ncol, nfield, nrow = background.shape
    block_cols = ncol // lax.axis_size("member")
    col_start = lax.axis_index("member") * block_cols

    mem = alpha.shape[0]
    cols_b = jnp.broadcast_to(loc_cols, (mem,) + loc_cols.shape)
    rows_b = jnp.broadcast_to(loc_rows, (mem,) + loc_rows.shape)

    def batched(lhs_dim, rhs_dim):
        return (((lhs_dim,), (rhs_dim,)), ((0,), (0,)))

    localized = lax.dot_general(cols_b, alpha, batched(2, 1), precision=highest)
    localized = lax.dot_general(localized, rows_b, batched(2, 2), precision=highest)
    ens = ensemble.astype(jnp.float32)
    partial = jnp.sum(ens * localized[:, :, None, :], axis=0)
    scattered = member_scatter(partial.transpose(1, 0, 2).reshape(nfield * ncol, nrow))

    meas = [measured_values[:, i] for i in range(nfield)]
    prec = [precision_factor[:, i] for i in range(nfield)]
    fixed = meas + prec + [depth]

    picked = jnp.concatenate([jnp.arange(2 * HALO), jnp.arange(nrow - 2 * HALO, nrow)])
    select = (picked[:, None] == jnp.arange(nrow)[None, :]).astype(jnp.float32)

    def ends(planes):
        cut = lax.dot_general(select, jnp.stack(planes), (((1,), (2,)), ((), ())),
                              precision=highest).transpose(1, 0, 2)
        return cut[:, : 2 * HALO], cut[:, 2 * HALO:]

    scattered, fixed_lo, fixed_hi = lax.optimization_barrier((scattered,) + ends(fixed))
    incr = member_gather(*scattered).reshape(nfield, ncol, nrow)
    state = [background[:, i] + incr[i] for i in range(nfield)]
    state_lo, state_hi = ends(state)
    own_lo = jnp.concatenate([state_lo, fixed_lo], axis=0)
    own_hi = jnp.concatenate([state_hi, fixed_hi], axis=0)
    before, after = shift_rows(None, (own_lo[:, :HALO], own_hi[:, HALO:]))

    pred, adj = block_dynamics(background.transpose(1, 0, 2), incr, measured_values.transpose(1, 0, 2),
                               precision_factor.transpose(1, 0, 2), depth)

    def strip(s):
        return dynamics(*s[:nfield], s[-1], s[2 * nfield:3 * nfield], s[nfield:2 * nfield],
                        col=2, row=1)

    both = strip(jnp.stack([jnp.concatenate([before, own_lo], axis=1),
                            jnp.concatenate([own_hi, after], axis=1)], axis=1))
    first = tuple(tuple(f[0] for f in part) for part in both)
    last = tuple(tuple(f[1] for f in part) for part in both)
    mid = slice(HALO, 2 * HALO)

    placed = jnp.concatenate([jnp.arange(HALO), jnp.arange(nrow - HALO, nrow)])
    place = (placed[:, None] == jnp.arange(nrow)[None, :]).astype(jnp.float32)
    at_edge = (jnp.arange(nrow) < HALO) | (jnp.arange(nrow) >= nrow - HALO)

    def assemble(k):
        rows = jnp.stack([jnp.concatenate([f[mid], g[mid]], axis=0)
                          for f, g in zip(first[k], last[k])])
        edge = lax.dot_general(rows, place, (((1,), (0,)), ((), ())), precision=highest)
        return jnp.stack([jnp.where(at_edge, edge[i], f) for i, f in enumerate((pred, adj)[k])],
                         axis=1)

    predicted_final = lax.dynamic_slice_in_dim(assemble(0), col_start, block_cols, 0)
    projected = jnp.sum(ens * assemble(1)[None], axis=2)
    rows_done = lax.dot_general(projected, rows_b, batched(2, 1), precision=highest)
    cost_derivative = alpha + lax.dot_general(cols_b, rows_done, batched(1, 1), precision=highest)
    return (cost_derivative, predicted_final)


def solution(mesh):
    return jax.shard_map(
        body,
        mesh=mesh,
        in_specs=(
            P("member", None, "tile"),
            P("member", None, None, "tile"),
            P(None, None, "tile"),
            P(None, None, "tile"),
            P(None, None, "tile"),
            P(None, "tile"),
            P(),
            P(),
        ),
        out_specs=(P("member", None, "tile"), P("member", None, "tile")),
        check_vma=False,
    )
```

```python
import jax
import jax.numpy as jnp
from jax import lax
from jax.experimental import pallas as pl
from jax.experimental.pallas import tpu as pltpu
from jax.sharding import PartitionSpec as P

STEPS = 2
COURANT = 0.3
HALO = 4 * STEPS


def shift_rows(x, sides):
    count = lax.axis_size("tile")
    up = [(i, (i + 1) % count) for i in range(count)]
    down = [(j, i) for i, j in up]
    lo, hi = sides
    before = lax.ppermute(hi, "tile", up)
    after = lax.ppermute(lo, "tile", down)
    return before, after


def jnp_slope(f, axis):
    return 0.5 * (jnp.roll(f, -1, axis) - jnp.roll(f, 1, axis))


def kernel_slope(f, axis):
    return 0.5 * (pltpu.roll(f, f.shape[axis] - 1, axis) - pltpu.roll(f, 1, axis))


def dynamics(h, u, v, dep, prec, meas, col=0, row=1, slope=jnp_slope):
    for _ in range(STEPS):
        h = h - COURANT * dep * (slope(u, col) + slope(v, row))
        u = u - COURANT * slope(h, col)
        v = v - COURANT * slope(h, row)
    pred = (h, u, v)
    a, p, q = (prec[i] * (pred[i] - meas[i]) for i in range(3))
    for _ in range(STEPS):
        e = a + COURANT * (slope(p, col) + slope(q, row))
        w = dep * e
        p = p + COURANT * slope(w, col)
        q = q + COURANT * slope(w, row)
        a = e
    return pred, (a, p, q)


def block_kernel(back_ref, incr_ref, meas_ref, prec_ref, dep_ref, pred_ref, adj_ref):
    count = back_ref.shape[0]
    pred, adj = dynamics(*(back_ref[i] + incr_ref[i] for i in range(count)), dep_ref[...],
                         [prec_ref[i] for i in range(count)], [meas_ref[i] for i in range(count)],
                         slope=kernel_slope)
    for i in range(count):
        pred_ref[i] = pred[i]
        adj_ref[i] = adj[i]


def block_dynamics(back, incr, meas, prec, dep):
    vmem = pl.BlockSpec(memory_space=pltpu.VMEM)
    out = jax.ShapeDtypeStruct(back.shape, back.dtype)
    return pl.pallas_call(
        block_kernel,
        out_shape=(out, out),
        in_specs=[vmem] * 5,
        out_specs=(vmem, vmem),
        cost_estimate=pl.CostEstimate(
            flops=120 * back.size, transcendentals=0, bytes_accessed=4 * (7 * back.size + dep.size)),
    )(back, incr, meas, prec, dep)


def member_scatter(x):
    count = lax.axis_size("member")
    me = lax.axis_index("member")
    rows, lanes = x.shape
    piece = -(-rows // (8 * count)) * 8
    x = jnp.pad(x, ((0, piece * count - rows), (0, 0))).reshape(count, piece, lanes)
    acc = lax.dynamic_index_in_dim(x, me, 0, keepdims=False)
    for s in range(1, count):
        shift = [(i, (i + s) % count) for i in range(count)]
        sent = lax.dynamic_index_in_dim(x, (me + s) % count, 0, keepdims=False)
        acc = acc + lax.ppermute(sent, "member", shift)
    return acc, jnp.zeros((rows,), x.dtype)


def member_gather(acc, like):
    count = lax.axis_size("member")
    me = lax.axis_index("member")
    out = jnp.zeros((count,) + acc.shape, acc.dtype)
    out = lax.dynamic_update_index_in_dim(out, acc, me, 0)
    for s in range(1, count):
        shift = [(i, (i + s) % count) for i in range(count)]
        got = lax.ppermute(acc, "member", shift)
        out = lax.dynamic_update_index_in_dim(out, got, (me + count - s) % count, 0)
    return out.reshape(count * acc.shape[0], acc.shape[1])[: like.shape[0]]


def member_gather_sum(x):
    count = lax.axis_size("member")
    me = lax.axis_index("member")
    pieces = [None] * count
    pieces[0] = x
    for s in range(1, count):
        shift = [(i, (i + s) % count) for i in range(count)]
        pieces[s] = lax.ppermute(x, "member", shift)
    total = None
    for src in range(count):
        term = pieces[0]
        for s in range(1, count):
            term = jnp.where((me + count - s) % count == src, pieces[s], term)
        total = term if total is None else total + term
    return total


def body(alpha, ensemble, background, measured_values, precision_factor, depth, loc_cols, loc_rows):
    highest = lax.Precision.HIGHEST
    ncol, nfield, nrow = background.shape
    block_cols = ncol // lax.axis_size("member")
    col_start = lax.axis_index("member") * block_cols

    mem = alpha.shape[0]
    cols_b = jnp.broadcast_to(loc_cols, (mem,) + loc_cols.shape)
    rows_b = jnp.broadcast_to(loc_rows, (mem,) + loc_rows.shape)

    def batched(lhs_dim, rhs_dim):
        return (((lhs_dim,), (rhs_dim,)), ((0,), (0,)))

    localized = lax.dot_general(cols_b, alpha, batched(2, 1), precision=highest)
    localized = lax.dot_general(localized, rows_b, batched(2, 2), precision=highest)
    ens = ensemble.astype(jnp.float32)
    partial = jnp.sum(ens * localized[:, :, None, :], axis=0)
    scattered = member_scatter(partial.transpose(1, 0, 2).reshape(nfield * ncol, nrow))

    meas = [measured_values[:, i] for i in range(nfield)]
    prec = [precision_factor[:, i] for i in range(nfield)]
    fixed = meas + prec + [depth]

    picked = jnp.concatenate([jnp.arange(2 * HALO), jnp.arange(nrow - 2 * HALO, nrow)])
    select = (picked[:, None] == jnp.arange(nrow)[None, :]).astype(jnp.float32)

    def ends(planes):
        cut = lax.dot_general(select, jnp.stack(planes), (((1,), (2,)), ((), ())),
                              precision=highest).transpose(1, 0, 2)
        return cut[:, : 2 * HALO], cut[:, 2 * HALO:]

    fixed_lo, fixed_hi = ends(fixed)
    fixed_before, fixed_after = shift_rows(None, (fixed_lo[:, :HALO], fixed_hi[:, HALO:]))
    scattered, fixed_lo, fixed_hi, fixed_before, fixed_after = lax.optimization_barrier(
        (scattered, fixed_lo, fixed_hi, fixed_before, fixed_after))
    incr = member_gather(*scattered).reshape(nfield, ncol, nrow)
    state = [background[:, i] + incr[i] for i in range(nfield)]
    state_lo, state_hi = ends(state)
    own_lo = jnp.concatenate([state_lo, fixed_lo], axis=0)
    own_hi = jnp.concatenate([state_hi, fixed_hi], axis=0)
    state_before, state_after = shift_rows(None, (state_lo[:, :HALO], state_hi[:, HALO:]))
    before = jnp.concatenate([state_before, fixed_before], axis=0)
    after = jnp.concatenate([state_after, fixed_after], axis=0)

    pred, adj = block_dynamics(background.transpose(1, 0, 2), incr, measured_values.transpose(1, 0, 2),
                               precision_factor.transpose(1, 0, 2), depth)

    def strip(s):
        return dynamics(*s[:nfield], s[-1], s[2 * nfield:3 * nfield], s[nfield:2 * nfield],
                        col=2, row=1)

    both = strip(jnp.stack([jnp.concatenate([before, own_lo], axis=1),
                            jnp.concatenate([own_hi, after], axis=1)], axis=1))
    first = tuple(tuple(f[0] for f in part) for part in both)
    last = tuple(tuple(f[1] for f in part) for part in both)
    mid = slice(HALO, 2 * HALO)

    placed = jnp.concatenate([jnp.arange(HALO), jnp.arange(nrow - HALO, nrow)])
    place = (placed[:, None] == jnp.arange(nrow)[None, :]).astype(jnp.float32)
    at_edge = (jnp.arange(nrow) < HALO) | (jnp.arange(nrow) >= nrow - HALO)

    def assemble(k):
        rows = jnp.stack([jnp.concatenate([f[mid], g[mid]], axis=0)
                          for f, g in zip(first[k], last[k])])
        edge = lax.dot_general(rows, place, (((1,), (0,)), ((), ())), precision=highest)
        return jnp.stack([jnp.where(at_edge, edge[i], f) for i, f in enumerate((pred, adj)[k])],
                         axis=1)

    predicted_final = lax.dynamic_slice_in_dim(assemble(0), col_start, block_cols, 0)
    projected = jnp.sum(ens * assemble(1)[None], axis=2)
    rows_done = lax.dot_general(projected, rows_b, batched(2, 1), precision=highest)
    cost_derivative = alpha + lax.dot_general(cols_b, rows_done, batched(1, 1), precision=highest)
    return (cost_derivative, predicted_final)


def solution(mesh):
    return jax.shard_map(
        body,
        mesh=mesh,
        in_specs=(
            P("member", None, "tile"),
            P("member", None, None, "tile"),
            P(None, None, "tile"),
            P(None, None, "tile"),
            P(None, None, "tile"),
            P(None, "tile"),
            P(),
            P(),
        ),
        out_specs=(P("member", None, "tile"), P("member", None, "tile")),
        check_vma=False,
    )
```

```python
import jax
import jax.numpy as jnp
from jax import lax
from jax.experimental import pallas as pl
from jax.experimental.pallas import tpu as pltpu
from jax.sharding import PartitionSpec as P

STEPS = 2
COURANT = 0.3
HALO = 4 * STEPS


def shift_rows(x, sides):
    count = lax.axis_size("tile")
    up = [(i, (i + 1) % count) for i in range(count)]
    down = [(j, i) for i, j in up]
    lo, hi = sides
    before = lax.ppermute(hi, "tile", up)
    after = lax.ppermute(lo, "tile", down)
    return before, after


def jnp_slope(f, axis):
    return 0.5 * (jnp.roll(f, -1, axis) - jnp.roll(f, 1, axis))


def kernel_slope(f, axis):
    return 0.5 * (pltpu.roll(f, f.shape[axis] - 1, axis) - pltpu.roll(f, 1, axis))


def dynamics(h, u, v, dep, prec, meas, col=0, row=1, slope=jnp_slope):
    for _ in range(STEPS):
        h = h - COURANT * dep * (slope(u, col) + slope(v, row))
        u = u - COURANT * slope(h, col)
        v = v - COURANT * slope(h, row)
    pred = (h, u, v)
    a, p, q = (prec[i] * (pred[i] - meas[i]) for i in range(3))
    for _ in range(STEPS):
        e = a + COURANT * (slope(p, col) + slope(q, row))
        w = dep * e
        p = p + COURANT * slope(w, col)
        q = q + COURANT * slope(w, row)
        a = e
    return pred, (a, p, q)


def block_kernel(back_ref, incr_ref, meas_ref, prec_ref, dep_ref, pred_ref, adj_ref):
    count = back_ref.shape[0]
    pred, adj = dynamics(*(back_ref[i] + incr_ref[i] for i in range(count)), dep_ref[...],
                         [prec_ref[i] for i in range(count)], [meas_ref[i] for i in range(count)],
                         slope=kernel_slope)
    for i in range(count):
        pred_ref[i] = pred[i]
        adj_ref[i] = adj[i]


def block_dynamics(back, incr, meas, prec, dep):
    vmem = pl.BlockSpec(memory_space=pltpu.VMEM)
    out = jax.ShapeDtypeStruct(back.shape, back.dtype)
    return pl.pallas_call(
        block_kernel,
        out_shape=(out, out),
        in_specs=[vmem] * 5,
        out_specs=(vmem, vmem),
        cost_estimate=pl.CostEstimate(
            flops=120 * back.size, transcendentals=0, bytes_accessed=4 * (7 * back.size + dep.size)),
    )(back, incr, meas, prec, dep)


def member_scatter(x):
    count = lax.axis_size("member")
    me = lax.axis_index("member")
    rows, lanes = x.shape
    piece = -(-rows // (8 * count)) * 8
    x = jnp.pad(x, ((0, piece * count - rows), (0, 0))).reshape(count, piece, lanes)
    acc = lax.dynamic_index_in_dim(x, me, 0, keepdims=False)
    for s in range(1, count):
        shift = [(i, (i + s) % count) for i in range(count)]
        sent = lax.dynamic_index_in_dim(x, (me + s) % count, 0, keepdims=False)
        acc = acc + lax.ppermute(sent, "member", shift)
    return acc, jnp.zeros((rows,), x.dtype)


def member_gather(acc, like):
    count = lax.axis_size("member")
    me = lax.axis_index("member")
    out = jnp.zeros((count,) + acc.shape, acc.dtype)
    out = lax.dynamic_update_index_in_dim(out, acc, me, 0)
    for s in range(1, count):
        shift = [(i, (i + s) % count) for i in range(count)]
        got = lax.ppermute(acc, "member", shift)
        out = lax.dynamic_update_index_in_dim(out, got, (me + count - s) % count, 0)
    return out.reshape(count * acc.shape[0], acc.shape[1])[: like.shape[0]]


def member_gather_sum(x):
    count = lax.axis_size("member")
    me = lax.axis_index("member")
    pieces = [None] * count
    pieces[0] = x
    for s in range(1, count):
        shift = [(i, (i + s) % count) for i in range(count)]
        pieces[s] = lax.ppermute(x, "member", shift)
    total = None
    for src in range(count):
        term = pieces[0]
        for s in range(1, count):
            term = jnp.where((me + count - s) % count == src, pieces[s], term)
        total = term if total is None else total + term
    return total


def body(alpha, ensemble, background, measured_values, precision_factor, depth, loc_cols, loc_rows):
    highest = lax.Precision.HIGHEST
    high = lax.Precision.HIGH
    ncol, nfield, nrow = background.shape
    block_cols = ncol // lax.axis_size("member")
    col_start = lax.axis_index("member") * block_cols

    mem = alpha.shape[0]
    cols_b = jnp.broadcast_to(loc_cols, (mem,) + loc_cols.shape)
    rows_b = jnp.broadcast_to(loc_rows, (mem,) + loc_rows.shape)

    def batched(lhs_dim, rhs_dim):
        return (((lhs_dim,), (rhs_dim,)), ((0,), (0,)))

    localized = lax.dot_general(cols_b, alpha, batched(2, 1), precision=high)
    localized = lax.dot_general(localized, rows_b, batched(2, 2), precision=high)
    ens = ensemble.astype(jnp.float32)
    partial = jnp.sum(ens * localized[:, :, None, :], axis=0)
    scattered = member_scatter(partial.transpose(1, 0, 2).reshape(nfield * ncol, nrow))

    meas = [measured_values[:, i] for i in range(nfield)]
    prec = [precision_factor[:, i] for i in range(nfield)]
    fixed = meas + prec + [depth]

    picked = jnp.concatenate([jnp.arange(2 * HALO), jnp.arange(nrow - 2 * HALO, nrow)])
    select = (picked[:, None] == jnp.arange(nrow)[None, :]).astype(jnp.float32)

    def ends(planes):
        cut = lax.dot_general(select, jnp.stack(planes), (((1,), (2,)), ((), ())),
                              precision=highest).transpose(1, 0, 2)
        return cut[:, : 2 * HALO], cut[:, 2 * HALO:]

    scattered, fixed_lo, fixed_hi = lax.optimization_barrier((scattered,) + ends(fixed))
    incr = member_gather(*scattered).reshape(nfield, ncol, nrow)
    state = [background[:, i] + incr[i] for i in range(nfield)]
    state_lo, state_hi = ends(state)
    own_lo = jnp.concatenate([state_lo, fixed_lo], axis=0)
    own_hi = jnp.concatenate([state_hi, fixed_hi], axis=0)
    before, after = shift_rows(None, (own_lo[:, :HALO], own_hi[:, HALO:]))

    pred, adj = block_dynamics(background.transpose(1, 0, 2), incr, measured_values.transpose(1, 0, 2),
                               precision_factor.transpose(1, 0, 2), depth)

    def strip(s):
        return dynamics(*s[:nfield], s[-1], s[2 * nfield:3 * nfield], s[nfield:2 * nfield],
                        col=2, row=1)

    both = strip(jnp.stack([jnp.concatenate([before, own_lo], axis=1),
                            jnp.concatenate([own_hi, after], axis=1)], axis=1))
    first = tuple(tuple(f[0] for f in part) for part in both)
    last = tuple(tuple(f[1] for f in part) for part in both)
    mid = slice(HALO, 2 * HALO)

    placed = jnp.concatenate([jnp.arange(HALO), jnp.arange(nrow - HALO, nrow)])
    place = (placed[:, None] == jnp.arange(nrow)[None, :]).astype(jnp.float32)
    at_edge = (jnp.arange(nrow) < HALO) | (jnp.arange(nrow) >= nrow - HALO)

    def assemble(k):
        rows = jnp.stack([jnp.concatenate([f[mid], g[mid]], axis=0)
                          for f, g in zip(first[k], last[k])])
        edge = lax.dot_general(rows, place, (((1,), (0,)), ((), ())), precision=highest)
        return jnp.stack([jnp.where(at_edge, edge[i], f) for i, f in enumerate((pred, adj)[k])],
                         axis=1)

    predicted_final = lax.dynamic_slice_in_dim(assemble(0), col_start, block_cols, 0)
    projected = jnp.sum(ens * assemble(1)[None], axis=2)
    rows_done = lax.dot_general(projected, rows_b, batched(2, 1), precision=high)
    cost_derivative = alpha + lax.dot_general(cols_b, rows_done, batched(1, 1), precision=high)
    return (cost_derivative, predicted_final)


def solution(mesh):
    return jax.shard_map(
        body,
        mesh=mesh,
        in_specs=(
            P("member", None, "tile"),
            P("member", None, None, "tile"),
            P(None, None, "tile"),
            P(None, None, "tile"),
            P(None, None, "tile"),
            P(None, "tile"),
            P(),
            P(),
        ),
        out_specs=(P("member", None, "tile"), P("member", None, "tile")),
        check_vma=False,
    )
```

```python
import jax
import jax.numpy as jnp
from jax import lax
from jax.experimental import pallas as pl
from jax.experimental.pallas import tpu as pltpu
from jax.sharding import PartitionSpec as P

STEPS = 2
COURANT = 0.3
HALO = 4 * STEPS


def shift_rows(x, sides):
    count = lax.axis_size("tile")
    up = [(i, (i + 1) % count) for i in range(count)]
    down = [(j, i) for i, j in up]
    lo, hi = sides
    before = lax.ppermute(hi, "tile", up)
    after = lax.ppermute(lo, "tile", down)
    return before, after


def jnp_slope(f, axis):
    return 0.5 * (jnp.roll(f, -1, axis) - jnp.roll(f, 1, axis))


def kernel_slope(f, axis):
    return 0.5 * (pltpu.roll(f, f.shape[axis] - 1, axis) - pltpu.roll(f, 1, axis))


def dynamics(h, u, v, dep, prec, meas, col=0, row=1, slope=jnp_slope):
    for _ in range(STEPS):
        h = h - COURANT * dep * (slope(u, col) + slope(v, row))
        u = u - COURANT * slope(h, col)
        v = v - COURANT * slope(h, row)
    pred = (h, u, v)
    a, p, q = (prec[i] * (pred[i] - meas[i]) for i in range(3))
    for _ in range(STEPS):
        e = a + COURANT * (slope(p, col) + slope(q, row))
        w = dep * e
        p = p + COURANT * slope(w, col)
        q = q + COURANT * slope(w, row)
        a = e
    return pred, (a, p, q)


def block_kernel(back_ref, incr_ref, meas_ref, prec_ref, dep_ref, pred_ref, adj_ref):
    count = back_ref.shape[0]
    pred, adj = dynamics(*(back_ref[i] + incr_ref[i] for i in range(count)), dep_ref[...],
                         [prec_ref[i] for i in range(count)], [meas_ref[i] for i in range(count)],
                         slope=kernel_slope)
    for i in range(count):
        pred_ref[i] = pred[i]
        adj_ref[i] = adj[i]


def block_dynamics(back, incr, meas, prec, dep):
    vmem = pl.BlockSpec(memory_space=pltpu.VMEM)
    out = jax.ShapeDtypeStruct(back.shape, back.dtype)
    return pl.pallas_call(
        block_kernel,
        out_shape=(out, out),
        in_specs=[vmem] * 5,
        out_specs=(vmem, vmem),
        cost_estimate=pl.CostEstimate(
            flops=120 * back.size, transcendentals=0, bytes_accessed=4 * (7 * back.size + dep.size)),
    )(back, incr, meas, prec, dep)


def member_scatter(x):
    count = lax.axis_size("member")
    me = lax.axis_index("member")
    rows, lanes = x.shape
    piece = -(-rows // (8 * count)) * 8
    x = jnp.pad(x, ((0, piece * count - rows), (0, 0))).reshape(count, piece, lanes)
    acc = lax.dynamic_index_in_dim(x, me, 0, keepdims=False)
    for s in range(1, count):
        shift = [(i, (i + s) % count) for i in range(count)]
        sent = lax.dynamic_index_in_dim(x, (me + s) % count, 0, keepdims=False)
        acc = acc + lax.ppermute(sent, "member", shift)
    return acc, jnp.zeros((rows,), x.dtype)


def member_gather(acc, like):
    count = lax.axis_size("member")
    me = lax.axis_index("member")
    out = jnp.zeros((count,) + acc.shape, acc.dtype)
    out = lax.dynamic_update_index_in_dim(out, acc, me, 0)
    for s in range(1, count):
        shift = [(i, (i + s) % count) for i in range(count)]
        got = lax.ppermute(acc, "member", shift)
        out = lax.dynamic_update_index_in_dim(out, got, (me + count - s) % count, 0)
    return out.reshape(count * acc.shape[0], acc.shape[1])[: like.shape[0]]


def member_gather_sum(x):
    count = lax.axis_size("member")
    me = lax.axis_index("member")
    pieces = [None] * count
    pieces[0] = x
    for s in range(1, count):
        shift = [(i, (i + s) % count) for i in range(count)]
        pieces[s] = lax.ppermute(x, "member", shift)
    total = None
    for src in range(count):
        term = pieces[0]
        for s in range(1, count):
            term = jnp.where((me + count - s) % count == src, pieces[s], term)
        total = term if total is None else total + term
    return total


def body(alpha, ensemble, background, measured_values, precision_factor, depth, loc_cols, loc_rows):
    high = lax.Precision.HIGH
    ncol, nfield, nrow = background.shape
    block_cols = ncol // lax.axis_size("member")
    col_start = lax.axis_index("member") * block_cols

    mem = alpha.shape[0]
    cols_b = jnp.broadcast_to(loc_cols, (mem,) + loc_cols.shape)
    rows_b = jnp.broadcast_to(loc_rows, (mem,) + loc_rows.shape)

    def batched(lhs_dim, rhs_dim):
        return (((lhs_dim,), (rhs_dim,)), ((0,), (0,)))

    localized = lax.dot_general(cols_b, alpha, batched(2, 1), precision=high)
    localized = lax.dot_general(localized, rows_b, batched(2, 2), precision=high)
    ens = ensemble.astype(jnp.float32)
    partial = jnp.sum(ens * localized[:, :, None, :], axis=0)
    scattered = member_scatter(partial.transpose(1, 0, 2).reshape(nfield * ncol, nrow))

    meas = [measured_values[:, i] for i in range(nfield)]
    prec = [precision_factor[:, i] for i in range(nfield)]
    fixed = meas + prec + [depth]

    picked = jnp.concatenate([jnp.arange(2 * HALO), jnp.arange(nrow - 2 * HALO, nrow)])
    select = (picked[:, None] == jnp.arange(nrow)[None, :]).astype(jnp.float32)

    def ends(planes):
        cut = lax.dot_general(select, jnp.stack(planes), (((1,), (2,)), ((), ())),
                              precision=high).transpose(1, 0, 2)
        return cut[:, : 2 * HALO], cut[:, 2 * HALO:]

    scattered, fixed_lo, fixed_hi = lax.optimization_barrier((scattered,) + ends(fixed))
    incr = member_gather(*scattered).reshape(nfield, ncol, nrow)
    state = [background[:, i] + incr[i] for i in range(nfield)]
    state_lo, state_hi = ends(state)
    own_lo = jnp.concatenate([state_lo, fixed_lo], axis=0)
    own_hi = jnp.concatenate([state_hi, fixed_hi], axis=0)
    before, after = shift_rows(None, (own_lo[:, :HALO], own_hi[:, HALO:]))

    pred, adj = block_dynamics(background.transpose(1, 0, 2), incr, measured_values.transpose(1, 0, 2),
                               precision_factor.transpose(1, 0, 2), depth)

    def strip(s):
        return dynamics(*s[:nfield], s[-1], s[2 * nfield:3 * nfield], s[nfield:2 * nfield],
                        col=2, row=1)

    both = strip(jnp.stack([jnp.concatenate([before, own_lo], axis=1),
                            jnp.concatenate([own_hi, after], axis=1)], axis=1))
    first = tuple(tuple(f[0] for f in part) for part in both)
    last = tuple(tuple(f[1] for f in part) for part in both)
    mid = slice(HALO, 2 * HALO)

    placed = jnp.concatenate([jnp.arange(HALO), jnp.arange(nrow - HALO, nrow)])
    place = (placed[:, None] == jnp.arange(nrow)[None, :]).astype(jnp.float32)
    at_edge = (jnp.arange(nrow) < HALO) | (jnp.arange(nrow) >= nrow - HALO)

    def assemble(k):
        rows = jnp.stack([jnp.concatenate([f[mid], g[mid]], axis=0)
                          for f, g in zip(first[k], last[k])])
        edge = lax.dot_general(rows, place, (((1,), (0,)), ((), ())), precision=high)
        return jnp.stack([jnp.where(at_edge, edge[i], f) for i, f in enumerate((pred, adj)[k])],
                         axis=1)

    predicted_final = lax.dynamic_slice_in_dim(assemble(0), col_start, block_cols, 0)
    projected = jnp.sum(ens * assemble(1)[None], axis=2)
    rows_done = lax.dot_general(projected, rows_b, batched(2, 1), precision=high)
    cost_derivative = alpha + lax.dot_general(cols_b, rows_done, batched(1, 1), precision=high)
    return (cost_derivative, predicted_final)


def solution(mesh):
    return jax.shard_map(
        body,
        mesh=mesh,
        in_specs=(
            P("member", None, "tile"),
            P("member", None, None, "tile"),
            P(None, None, "tile"),
            P(None, None, "tile"),
            P(None, None, "tile"),
            P(None, "tile"),
            P(),
            P(),
        ),
        out_specs=(P("member", None, "tile"), P("member", None, "tile")),
        check_vma=False,
    )
```

```python
import jax
import jax.numpy as jnp
from jax import lax
from jax.experimental import pallas as pl
from jax.experimental.pallas import tpu as pltpu
from jax.sharding import PartitionSpec as P

STEPS = 2
COURANT = 0.3
HALO = 4 * STEPS


def shift_rows(x, sides):
    count = lax.axis_size("tile")
    up = [(i, (i + 1) % count) for i in range(count)]
    down = [(j, i) for i, j in up]
    lo, hi = sides
    before = lax.ppermute(hi, "tile", up)
    after = lax.ppermute(lo, "tile", down)
    return before, after


def jnp_slope(f, axis):
    return 0.5 * (jnp.roll(f, -1, axis) - jnp.roll(f, 1, axis))


def kernel_slope(f, axis):
    return 0.5 * (pltpu.roll(f, f.shape[axis] - 1, axis) - pltpu.roll(f, 1, axis))


def dynamics(h, u, v, dep, prec, meas, col=0, row=1, slope=jnp_slope):
    for _ in range(STEPS):
        h = h - COURANT * dep * (slope(u, col) + slope(v, row))
        u = u - COURANT * slope(h, col)
        v = v - COURANT * slope(h, row)
    pred = (h, u, v)
    a, p, q = (prec[i] * (pred[i] - meas[i]) for i in range(3))
    for _ in range(STEPS):
        e = a + COURANT * (slope(p, col) + slope(q, row))
        w = dep * e
        p = p + COURANT * slope(w, col)
        q = q + COURANT * slope(w, row)
        a = e
    return pred, (a, p, q)


def block_kernel(back_ref, incr_ref, meas_ref, prec_ref, dep_ref, pred_ref, adj_ref):
    count = back_ref.shape[0]
    pred, adj = dynamics(*(back_ref[i] + incr_ref[i] for i in range(count)), dep_ref[...],
                         [prec_ref[i] for i in range(count)], [meas_ref[i] for i in range(count)],
                         slope=kernel_slope)
    for i in range(count):
        pred_ref[i] = pred[i]
        adj_ref[i] = adj[i]


def block_dynamics(back, incr, meas, prec, dep):
    vmem = pl.BlockSpec(memory_space=pltpu.VMEM)
    out = jax.ShapeDtypeStruct(back.shape, back.dtype)
    return pl.pallas_call(
        block_kernel,
        out_shape=(out, out),
        in_specs=[vmem] * 5,
        out_specs=(vmem, vmem),
        cost_estimate=pl.CostEstimate(
            flops=120 * back.size, transcendentals=0, bytes_accessed=4 * (7 * back.size + dep.size)),
    )(back, incr, meas, prec, dep)


def member_scatter(x):
    count = lax.axis_size("member")
    me = lax.axis_index("member")
    rows, lanes = x.shape
    piece = -(-rows // (8 * count)) * 8
    x = jnp.pad(x, ((0, piece * count - rows), (0, 0))).reshape(count, piece, lanes)
    acc = lax.dynamic_index_in_dim(x, me, 0, keepdims=False)
    for s in range(1, count):
        shift = [(i, (i + s) % count) for i in range(count)]
        sent = lax.dynamic_index_in_dim(x, (me + s) % count, 0, keepdims=False)
        acc = acc + lax.ppermute(sent, "member", shift)
    return acc, jnp.zeros((rows,), x.dtype)


def member_gather(acc, like):
    count = lax.axis_size("member")
    me = lax.axis_index("member")
    out = jnp.zeros((count,) + acc.shape, acc.dtype)
    out = lax.dynamic_update_index_in_dim(out, acc, me, 0)
    for s in range(1, count):
        shift = [(i, (i + s) % count) for i in range(count)]
        got = lax.ppermute(acc, "member", shift)
        out = lax.dynamic_update_index_in_dim(out, got, (me + count - s) % count, 0)
    return out.reshape(count * acc.shape[0], acc.shape[1])[: like.shape[0]]


def member_gather_sum(x):
    count = lax.axis_size("member")
    me = lax.axis_index("member")
    pieces = [None] * count
    pieces[0] = x
    for s in range(1, count):
        shift = [(i, (i + s) % count) for i in range(count)]
        pieces[s] = lax.ppermute(x, "member", shift)
    total = None
    for src in range(count):
        term = pieces[0]
        for s in range(1, count):
            term = jnp.where((me + count - s) % count == src, pieces[s], term)
        total = term if total is None else total + term
    return total


def body(alpha, ensemble, background, measured_values, precision_factor, depth, loc_cols, loc_rows):
    highest = lax.Precision.HIGHEST
    high = lax.Precision.HIGH
    ncol, nfield, nrow = background.shape
    block_cols = ncol // lax.axis_size("member")
    col_start = lax.axis_index("member") * block_cols

    mem = alpha.shape[0]
    cols_b = jnp.broadcast_to(loc_cols, (mem,) + loc_cols.shape)
    rows_b = jnp.broadcast_to(loc_rows, (mem,) + loc_rows.shape)

    def batched(lhs_dim, rhs_dim):
        return (((lhs_dim,), (rhs_dim,)), ((0,), (0,)))

    localized = lax.dot_general(cols_b, alpha, batched(2, 1), precision=high)
    localized = lax.dot_general(localized, rows_b, batched(2, 2), precision=high)
    ens = ensemble.astype(jnp.float32)
    partial = jnp.sum(ens * localized[:, :, None, :], axis=0)
    scattered = member_scatter(partial.transpose(1, 0, 2).reshape(nfield * ncol, nrow))

    meas = [measured_values[:, i] for i in range(nfield)]
    prec = [precision_factor[:, i] for i in range(nfield)]
    fixed = meas + prec + [depth]

    picked = jnp.concatenate([jnp.arange(2 * HALO), jnp.arange(nrow - 2 * HALO, nrow)])
    select = (picked[:, None] == jnp.arange(nrow)[None, :]).astype(jnp.float32)

    def ends(planes):
        cut = lax.dot_general(select, jnp.stack(planes), (((1,), (2,)), ((), ())),
                              precision=highest).transpose(1, 0, 2)
        return cut[:, : 2 * HALO], cut[:, 2 * HALO:]

    scattered, fixed_lo, fixed_hi = lax.optimization_barrier((scattered,) + ends(fixed))
    incr = member_gather(*scattered).reshape(nfield, ncol, nrow)
    state = [background[:, i] + incr[i] for i in range(nfield)]
    state_lo, state_hi = ends(state)
    own_lo = jnp.concatenate([state_lo, fixed_lo], axis=0)
    own_hi = jnp.concatenate([state_hi, fixed_hi], axis=0)
    before, after = shift_rows(None, (own_lo[:, :HALO], own_hi[:, HALO:]))

    pred, adj = block_dynamics(background.transpose(1, 0, 2), incr, measured_values.transpose(1, 0, 2),
                               precision_factor.transpose(1, 0, 2), depth)

    def strip(s):
        return dynamics(*s[:nfield], s[-1], s[2 * nfield:3 * nfield], s[nfield:2 * nfield],
                        col=2, row=1)

    both = strip(jnp.stack([jnp.concatenate([before, own_lo], axis=1),
                            jnp.concatenate([own_hi, after], axis=1)], axis=1))
    first = tuple(tuple(f[0] for f in part) for part in both)
    last = tuple(tuple(f[1] for f in part) for part in both)
    mid = slice(HALO, 2 * HALO)

    placed = jnp.concatenate([jnp.arange(HALO), jnp.arange(nrow - HALO, nrow)])
    place = (placed[:, None] == jnp.arange(nrow)[None, :]).astype(jnp.float32)
    at_edge = (jnp.arange(nrow) < HALO) | (jnp.arange(nrow) >= nrow - HALO)

    rows = jnp.stack([jnp.concatenate([f[mid], g[mid]], axis=0)
                      for k in range(2) for f, g in zip(first[k], last[k])])
    edges = lax.dot_general(rows, place, (((1,), (0,)), ((), ())), precision=highest)

    def assemble(k):
        return jnp.stack([jnp.where(at_edge, edges[k * nfield + i], f)
                          for i, f in enumerate((pred, adj)[k])], axis=1)

    predicted_final = lax.dynamic_slice_in_dim(assemble(0), col_start, block_cols, 0)
    projected = jnp.sum(ens * assemble(1)[None], axis=2)
    rows_done = lax.dot_general(projected, rows_b, batched(2, 1), precision=high)
    cost_derivative = alpha + lax.dot_general(cols_b, rows_done, batched(1, 1), precision=high)
    return (cost_derivative, predicted_final)


def solution(mesh):
    return jax.shard_map(
        body,
        mesh=mesh,
        in_specs=(
            P("member", None, "tile"),
            P("member", None, None, "tile"),
            P(None, None, "tile"),
            P(None, None, "tile"),
            P(None, None, "tile"),
            P(None, "tile"),
            P(),
            P(),
        ),
        out_specs=(P("member", None, "tile"), P("member", None, "tile")),
        check_vma=False,
    )
```
